512 devices in a mesh: seq: 64 (over z_hi, y, core), tp: 8 (over x, z_lo).
Axes of the slice: x: 4, y: 8, z: 8 (z_hi: 4, z_lo: 2; z = z_hi * 2 + z_lo), core: 2. Of those that a mesh axis runs over, the one named last changes fastest.
Arguments:
- query_proj: bfloat16 [16384, 3072], P('seq', 'tp'), may hold values from -8 to 8
- key_proj: bfloat16 [16384, 3072], P('seq', 'tp'), may hold values from -8 to 8
- value_proj: bfloat16 [16384, 3072], P('seq', 'tp'), may hold values from -6 to 6
- hidden: bfloat16 [16384, 3072], P('seq', 'tp'), may hold values from -2 to 2
- out_weight: bfloat16 [3072, 3072], P('tp'), may hold values from -0.109375 to 0.109375
- norm_gain: bfloat16 [3072], P('tp'), may hold values from 0.099609375 to 1.8984375
- segment_ids: int32 [16384], P('seq'), may hold values from 0 to 31, never falling along the last dimension, each value on 1 to 8192 neighbouring positions
- pad_mask: int32 [16384], P('seq'), may hold values 0 or 1
- page_table: int32 [128], P('seq'), may hold values from 0 to 1, as said below
Outputs:
- hidden_out: bfloat16 [16384, 3072], P('seq', 'tp')
- normed: bfloat16 [16384, 3072], P('seq', 'tp')
- kv_pages: bfloat16 [128, 2, 128, 3072], P('seq', None, None, 'tp')
The draws below stay inside these ranges and needn't reach their ends.
Inputs may be any that keep to these rules, and one draw needn't show every extreme that they name: `segment_ids`: never falling along the tokens; each of the 32 prompts has 1 to 8192 tokens, one exactly 8192. `page_table`: the 2 pages of each aligned block of 2 pages name each slot once.
All inputs are finite; a program needn't handle non-finite values. No bound on the sum of `pad_mask` on one device may be relied on, other than what follows from the above.
Results may differ from the reference program's by a relative error of at most 0.014.
Values may be sent and summed in bfloat16 or wider, within the bound.
No kernel may reach another device: no remote copies, remote signals or barrier semaphores. Data moves between devices by JAX's collectives and lax.ppermute only.
A program may use at most 128 MiB of HBM per device.

```python
import math
import jax
import jax.numpy as jnp
import numpy as np
from jax import lax

D = 3072
HEADS = 32
HEAD_DIM = 96
TOK_DEV = 256
PAGE = 128
TOKENS = 16384
SEG_MOST = 8192
SEGS = 32
PAGES = 128
PAGES_DEV = 2


def query_and_key(key):
    base = jax.random.fold_in(key, 11)
    key_query, key_keys = jax.random.split(base, 2)
    width_all = HEADS * HEAD_DIM
    q_values = jnp.clip(jax.random.normal(key_query, (TOKENS, width_all), jnp.float32), -6.0, 6.0)
    k_values = jnp.clip(jax.random.normal(key_keys, (TOKENS, width_all), jnp.float32), -6.0, 6.0)
    return (q_values, k_values)


def draw_query_proj(key, part):
    return query_and_key(key)[0].astype(jnp.bfloat16)


def draw_key_proj(key, part):
    return query_and_key(key)[1].astype(jnp.bfloat16)


def draw_hidden(key, part):
    key_main, key_rows, key_cols = jax.random.split(jax.random.fold_in(key, 23), 3)
    column = jnp.arange(D).astype(jnp.float32) / D
    base_values = jnp.clip(jax.random.normal(key_main, (TOKENS, D), jnp.float32), -6.0, 6.0)
    rising = jnp.exp(jnp.log(3.0) * column)
    row_scale = jnp.exp(jnp.log(10.0) * jax.random.uniform(key_rows, (TOKENS,), jnp.float32))
    col_scale = jnp.exp(jnp.log(10.0) * jax.random.uniform(key_cols, (D,), jnp.float32)) * rising
    result = 0.005 * base_values * row_scale[:, None] * col_scale[None, :]
    return jnp.clip(result, -2.0, 2.0).astype(jnp.bfloat16)


def draw_page_table(key, part):
    scores = jax.random.randint(jax.random.fold_in(key, 31), (PAGES // PAGES_DEV, PAGES_DEV), 0, 1048576)
    scores = scores * PAGES_DEV + jnp.arange(PAGES_DEV, dtype=jnp.int32)[None, :]
    return jnp.argsort(scores, axis=1).astype(jnp.int32).reshape(PAGES)


def with_ends(entries, own_key, low, top_value):
    dims = entries.shape
    place = [jax.random.randint(jax.random.fold_in(own_key, axis), (), 0, dims[axis]) for axis in range(len(dims))]
    entries = entries.at[tuple(place)].set(low)
    longest = dims.index(max(dims))
    place[longest] = (place[longest] + 1) % dims[longest]
    return entries.at[tuple(place)].set(top_value)


def levels(key, extent, cuts, least, top_value):
    factor_of = 1.0
    for axis_at, blocks in cuts:
        draws = jax.random.uniform(jax.random.fold_in(jax.random.fold_in(key, 6), axis_at), (blocks,), jnp.float32, least / len(cuts), top_value / len(cuts))
        factor_of = factor_of * jnp.repeat(jnp.exp(draws), extent[axis_at] // blocks).reshape((-1,) + (1,) * (len(extent) - 1 - axis_at))
    return factor_of


def length_profile(count, total, bound, lean):
    portions = [(1 << 20) // math.isqrt(standing ** lean) + 1 for standing in range(2, count + 1)]
    rest, given = total - bound - (count - 1), [1] * (count - 1)
    while rest > 0:
        free = [i for i in range(count - 1) if given[i] < bound]
        pool, budget = sum([portions[i] for i in free]), rest
        for i in free:
            addition = min(bound - given[i], max(1, budget * portions[i] // pool), rest)
            given[i] = given[i] + addition
            rest = rest - addition
    return np.array([bound] + given)


def ragged_sizes(own_key, number_of, total, limit, lean):
    if number_of == 2:
        one = jax.random.randint(own_key, (), max(1, total - limit), min(limit, total - 1) + 1)
        return jnp.stack([one, total - one])
    sizes = jnp.asarray(length_profile(number_of, total, limit, lean), jnp.int32)
    twos = (number_of - 1) // 2
    giver, taker = sizes[1:1 + 2 * twos:2], sizes[2:2 + 2 * twos:2]
    room = jnp.minimum(giver - 1, limit - taker)
    moved = jax.random.randint(jax.random.fold_in(own_key, 1), (twos,), 0, 1 << 20) % (room + 1)
    sizes = sizes.at[1:1 + 2 * twos:2].set(giver - moved).at[2:2 + 2 * twos:2].set(taker + moved)
    return sizes[jax.random.permutation(jax.random.fold_in(own_key, 2), number_of)]


def noise(rng, dims, width, limit, pieces=(), kind=jnp.bfloat16):
    entries = jax.random.normal(rng, dims, jnp.float32) * width
    if len(pieces) > 0:
        entries = levels(rng, dims, pieces, -0.22, 0.18) * entries
    return jnp.clip(entries, min=-limit, max=limit).astype(kind)


def setup_inputs(seed: int = 0) -> dict:
    key_list = jax.random.split(jax.random.key(seed), 10)
    query_proj = draw_query_proj(jax.random.fold_in(key_list[9], 71), 0)
    key_proj = draw_key_proj(jax.random.fold_in(key_list[9], 71), 0)
    value_proj = noise(key_list[2], (TOKENS, HEADS * HEAD_DIM), 1.0, 6.0, ((0, 64), (1, 8)))
    hidden = draw_hidden(jax.random.fold_in(key_list[9], 71), 0)
    out_weight = noise(key_list[4], (HEADS * HEAD_DIM, D), (HEADS * HEAD_DIM) ** -0.5, 0.109375, ((0, 8),))
    norm_gain = jnp.clip(1.0 + 0.18 * jax.random.normal(key_list[5], (D,), jnp.float32), 0.099609375, 1.8984375).astype(jnp.bfloat16)
    segment_ids = jnp.searchsorted(jnp.cumsum(ragged_sizes(key_list[6], SEGS, TOKENS, SEG_MOST, 2)), jnp.arange(TOKENS), side="right").astype(jnp.int32)
    pad_mask = with_ends((jax.random.randint(key_list[7], (TOKENS,), 0, 8) < 7).astype(jnp.int32), jax.random.fold_in(key_list[7], 1), 0, 1)
    page_table = draw_page_table(jax.random.fold_in(key_list[9], 71), 0)
    return dict(query_proj=query_proj, key_proj=key_proj, value_proj=value_proj, hidden=hidden, out_weight=out_weight, norm_gain=norm_gain, segment_ids=segment_ids, pad_mask=pad_mask, page_table=page_table)


far_index = 1073741824
masked_score = -1e+30
norm_epsilon = 1e-05

def rotate(values_in, position, head_count, head_dim):
    count_rows = values_in.shape[0]
    half_dim = head_dim // 2
    frequency = jnp.exp(jnp.arange(half_dim, dtype=jnp.float32) * (-2.0 * math.log(10000.0) / head_dim))
    angles = position.astype(jnp.float32)[:, None] * frequency[None, :]
    cosine = jnp.cos(angles)[:, None, :]
    sine_part = jnp.sin(angles)[:, None, :]
    as_float = values_in.astype(jnp.float32).reshape(count_rows, head_count, head_dim)
    lower_half = as_float[..., :half_dim]
    upper_half = as_float[..., half_dim:]
    rotated = jnp.concatenate([lower_half * cosine - upper_half * sine_part, upper_half * cosine + lower_half * sine_part], axis=-1)
    return rotated.reshape(count_rows, head_count * head_dim).astype(jnp.bfloat16)

def reference(query_proj, key_proj, value_proj, hidden, out_weight, norm_gain, segment_ids, pad_mask, page_table):
    tok_index = jnp.arange(TOKENS, dtype=jnp.int32)
    member = segment_ids[:, None] == jnp.arange(SEGS, dtype=jnp.int32)[None, :]
    seg_start = lax.optimization_barrier(jnp.min(jnp.where(member, tok_index[:, None], far_index), axis=0))
    position = tok_index - lax.optimization_barrier(jnp.sum(jnp.where(member, seg_start[None, :], 0), axis=1))
    q_rot = rotate(query_proj, position, HEADS, HEAD_DIM)
    k_rot = rotate(key_proj, position, HEADS, HEAD_DIM)
    key_tag = jnp.where(pad_mask == 1, segment_ids + 1, 0)
    key_window = min(SEG_MOST + TOK_DEV, TOKENS)
    factor = 1.0 / math.sqrt(HEAD_DIM)

    def one_block(block_index):
        q_start = (block_index * TOK_DEV).astype(jnp.int32)
        k_start = jnp.clip(q_start + TOK_DEV - key_window, 0, TOKENS - key_window).astype(jnp.int32)
        query_heads = lax.dynamic_slice_in_dim(q_rot, q_start, TOK_DEV, 0).astype(jnp.float32).reshape(TOK_DEV, HEADS, HEAD_DIM)
        key_heads = lax.dynamic_slice_in_dim(k_rot, k_start, key_window, 0).astype(jnp.float32).reshape(key_window, HEADS, HEAD_DIM)
        val_heads = lax.dynamic_slice_in_dim(value_proj, k_start, key_window, 0).astype(jnp.float32).reshape(key_window, HEADS, HEAD_DIM)
        query_seg = lax.dynamic_slice_in_dim(segment_ids, q_start, TOK_DEV, 0)
        tags = lax.dynamic_slice_in_dim(key_tag, k_start, key_window, 0)
        query_pos = q_start + jnp.arange(TOK_DEV, dtype=jnp.int32)
        key_pos = k_start + jnp.arange(key_window, dtype=jnp.int32)
        visible = (tags[None, :] == query_seg[:, None] + 1) & (key_pos[None, :] <= query_pos[:, None]) | (key_pos[None, :] == query_pos[:, None])
        logits = jnp.einsum('qhd,khd->hqk', query_heads, key_heads) * factor
        logits = jnp.where(visible[None], logits, masked_score)
        row_peak = lax.optimization_barrier(jnp.max(logits, axis=-1, keepdims=True))
        unnormed = jnp.where(visible[None], jnp.exp(logits - row_peak), 0.0)
        denom = lax.optimization_barrier(jnp.sum(unnormed, axis=-1))
        weights = unnormed.astype(jnp.bfloat16)
        weighted = jnp.einsum('hqk,khd->qhd', weights.astype(jnp.float32), val_heads)
        result = weighted / jnp.transpose(denom)[:, :, None]
        return result.reshape(TOK_DEV, HEADS * HEAD_DIM).astype(jnp.bfloat16)
    attn = lax.map(one_block, jnp.arange(TOKENS // TOK_DEV, dtype=jnp.int32)).reshape(TOKENS, HEADS * HEAD_DIM)
    proj = jnp.dot(attn, out_weight, preferred_element_type=jnp.float32)
    hidden_out = (hidden.astype(jnp.float32) + proj).astype(jnp.bfloat16)
    stream_wide = hidden_out.astype(jnp.float32)
    mean_square = lax.optimization_barrier(jnp.mean(stream_wide * stream_wide, axis=1, keepdims=True))
    normed = (stream_wide * lax.rsqrt(mean_square + norm_epsilon) * norm_gain.astype(jnp.float32)[None, :]).astype(jnp.bfloat16)
    pad_scale = pad_mask.astype(jnp.bfloat16)[:, None]
    stacked = jnp.stack([k_rot * pad_scale, value_proj * pad_scale])
    stacked = stacked.reshape(2, PAGES, PAGE, HEADS * HEAD_DIM).transpose(1, 0, 2, 3)
    destination = jnp.arange(PAGES, dtype=jnp.int32) // PAGES_DEV * PAGES_DEV + page_table
    kv_pages = jnp.zeros_like(stacked).at[destination].set(stacked)
    return (hidden_out, normed, kv_pages)
```

```python
import math

import jax
import jax.numpy as jnp
from jax import lax
from jax.sharding import PartitionSpec as P

D = 3072
HEAD_DIM = 96
PAGE = 128


far_index = 1073741824
masked_score = -1e30
norm_epsilon = 1e-05


def passed_along(block, axis, distance):
    devices = range(lax.axis_size(axis))
    route = [(i - distance, i) for i in devices if i - distance in devices]
    return lax.ppermute(block, axis, route)


def rotate(values_in, position, head_count, head_dim):
    count_rows = values_in.shape[0]
    half_dim = head_dim // 2
    frequency = jnp.exp(
        jnp.arange(half_dim, dtype=jnp.float32) * (-2.0 * math.log(10000.0) / head_dim)
    )
    angles = position.astype(jnp.float32)[:, None] * frequency[None, :]
    cosine = jnp.cos(angles)[:, None, :]
    sine_part = jnp.sin(angles)[:, None, :]
    as_float = values_in.astype(jnp.float32).reshape(count_rows, head_count, head_dim)
    lower_half = as_float[..., :half_dim]
    upper_half = as_float[..., half_dim:]
    rotated = jnp.concatenate(
        [
            lower_half * cosine - upper_half * sine_part,
            upper_half * cosine + lower_half * sine_part,
        ],
        axis=-1,
    )
    return rotated.reshape(count_rows, head_count * head_dim).astype(jnp.bfloat16)


def attend(softmax_state, query_heads, block, visible):
    row_peak, row_total, weighted = softmax_state
    key_count = block.shape[1]
    head_count = query_heads.shape[1]
    key_heads = block[0].reshape(key_count, head_count, HEAD_DIM)
    val_heads = block[1].reshape(key_count, head_count, HEAD_DIM)
    factor = 1.0 / math.sqrt(HEAD_DIM)
    logits = (
        jnp.einsum("qhd,khd->hqk", query_heads, key_heads, preferred_element_type=jnp.float32)
        * factor
    )
    logits = jnp.where(visible[None], logits, masked_score)
    new_peak = jnp.maximum(row_peak, jnp.max(logits, axis=-1))
    rescale = jnp.exp(row_peak - new_peak)
    unnormed = jnp.where(visible[None], jnp.exp(logits - new_peak[..., None]), 0.0)
    row_total = row_total * rescale + jnp.sum(unnormed, axis=-1)
    weighted = weighted * rescale[..., None] + jnp.einsum(
        "hqk,khd->hqd", unnormed.astype(jnp.bfloat16), val_heads, preferred_element_type=jnp.float32
    )
    return (new_peak, row_total, weighted)


def per_device(
    query_proj,
    key_proj,
    value_proj,
    hidden,
    out_weight,
    norm_gain,
    segment_ids,
    pad_mask,
    page_table,
):
    tok_count = query_proj.shape[0]
    feat_count = query_proj.shape[1]
    head_count = feat_count // HEAD_DIM
    seg_count = lax.axis_size("seq") // 2
    reach_count = lax.axis_size("seq") // 2
    device_row = lax.axis_index("seq")
    tok_index = device_row * tok_count + jnp.arange(tok_count, dtype=jnp.int32)
    member = segment_ids[:, None] == jnp.arange(seg_count, dtype=jnp.int32)[None, :]
    local_first = jnp.min(jnp.where(member, tok_index[:, None], far_index), axis=0)
    first_tok = lax.pmin(local_first, "seq")
    position = tok_index - jnp.sum(jnp.where(member, first_tok[None, :], 0), axis=1)
    q_rot = rotate(query_proj, position, head_count, HEAD_DIM)
    k_rot = rotate(key_proj, position, head_count, HEAD_DIM)
    query_heads = q_rot.reshape(tok_count, head_count, HEAD_DIM)
    query_tag = segment_ids + 1
    key_tag = jnp.where(pad_mask == 1, segment_ids + 1, 0)
    tag_rows = -(-tok_count // feat_count)
    tag_block = jnp.pad(key_tag.astype(jnp.bfloat16), (0, tag_rows * feat_count - tok_count))
    own_block = jnp.concatenate(
        [k_rot, value_proj, tag_block.reshape(tag_rows, feat_count)], axis=0
    )
    offsets = jnp.arange(tok_count, dtype=jnp.int32)
    own_visible = (key_tag[None, :] == query_tag[:, None]) & (
        offsets[None, :] <= offsets[:, None]
    ) | (offsets[None, :] == offsets[:, None])
    softmax_state = (
        jnp.full((head_count, tok_count), masked_score, jnp.float32),
        jnp.zeros((head_count, tok_count), jnp.float32),
        jnp.zeros((head_count, tok_count, HEAD_DIM), jnp.float32),
    )
    softmax_state = attend(softmax_state, query_heads, jnp.stack([k_rot, value_proj]), own_visible)
    query_tag_wide = query_tag.astype(jnp.bfloat16)

    def visit_block(current, moved):
        pair = moved[: 2 * tok_count].reshape(2, tok_count, feat_count)
        moved_tags = moved[2 * tok_count :].reshape(-1)[:tok_count]
        visible = moved_tags[None, :] == query_tag_wide[:, None]
        return attend(current, query_heads, pair, visible)

    def cycle_turn(turn_index, loop_state):
        current, moved = loop_state
        following = passed_along(moved, "seq", 1)
        return (visit_block(current, moved), following)

    moved = passed_along(own_block, "seq", 1)
    softmax_state, moved = lax.fori_loop(0, reach_count - 1, cycle_turn, (softmax_state, moved))
    softmax_state = visit_block(softmax_state, moved)
    row_peak, row_total, weighted = softmax_state
    attn = (
        jnp.transpose(weighted / row_total[..., None], (1, 0, 2))
        .reshape(tok_count, feat_count)
        .astype(jnp.bfloat16)
    )
    partial_value = jnp.dot(attn, out_weight, preferred_element_type=jnp.float32)
    feature_width = hidden.shape[1]
    own_sum = lax.psum_scatter(
        partial_value.astype(jnp.bfloat16), "tp", scatter_dimension=1, tiled=True
    ).astype(jnp.float32)
    hidden_out = (hidden.astype(jnp.float32) + own_sum).astype(jnp.bfloat16)
    stream_wide = hidden_out.astype(jnp.float32)
    square_total = lax.psum(jnp.sum(stream_wide * stream_wide, axis=1), "tp")
    normed = (
        stream_wide
        * lax.rsqrt(square_total / D + norm_epsilon)[:, None]
        * norm_gain.astype(jnp.float32)[None, :]
    ).astype(jnp.bfloat16)
    pad_scale = pad_mask.astype(jnp.bfloat16)[:, None]
    page_count = tok_count // PAGE
    stacked = jnp.stack([k_rot * pad_scale, value_proj * pad_scale])
    stacked = stacked.reshape(2, page_count, PAGE, feat_count).transpose(1, 0, 2, 3)
    kv_pages = jnp.zeros_like(stacked).at[page_table].set(stacked)
    return (hidden_out, normed, kv_pages)


def solution(mesh):
    placed = (
        P("seq", "tp"),
        P("seq", "tp"),
        P("seq", "tp"),
        P("seq", "tp"),
        P("tp", None),
        P("tp"),
        P("seq"),
        P("seq"),
        P("seq"),
    )
    return jax.shard_map(
        per_device,
        mesh=mesh,
        in_specs=placed,
        out_specs=(P("seq", "tp"), P("seq", "tp"), P("seq", None, None, "tp")),
        check_vma=False,
    )
```

```python
import math

import jax
import jax.numpy as jnp
from jax import lax
from jax.sharding import Mesh, PartitionSpec as P

D = 3072
HEAD_DIM = 96
PAGE = 128


far_index = 1073741824
masked_score = -1e30
norm_epsilon = 1e-05


def passed_along(block, axis, distance):
    devices = range(lax.axis_size(axis))
    route = [(i - distance, i) for i in devices if i - distance in devices]
    return lax.ppermute(block, axis, route)


def rotate(values_in, position, head_count, head_dim):
    count_rows = values_in.shape[0]
    half_dim = head_dim // 2
    frequency = jnp.exp(
        jnp.arange(half_dim, dtype=jnp.float32) * (-2.0 * math.log(10000.0) / head_dim)
    )
    angles = position.astype(jnp.float32)[:, None] * frequency[None, :]
    cosine = jnp.cos(angles)[:, None, :]
    sine_part = jnp.sin(angles)[:, None, :]
    as_float = values_in.astype(jnp.float32).reshape(count_rows, head_count, head_dim)
    lower_half = as_float[..., :half_dim]
    upper_half = as_float[..., half_dim:]
    rotated = jnp.concatenate(
        [
            lower_half * cosine - upper_half * sine_part,
            upper_half * cosine + lower_half * sine_part,
        ],
        axis=-1,
    )
    return rotated.reshape(count_rows, head_count * head_dim).astype(jnp.bfloat16)


def attend(softmax_state, query_heads, key_heads, val_heads, visible):
    row_peak, row_total, weighted = softmax_state
    factor = 1.0 / math.sqrt(HEAD_DIM)
    logits = (
        jnp.einsum("qd,kd->qk", query_heads, key_heads, preferred_element_type=jnp.float32)
        * factor
    )
    logits = jnp.where(visible, logits, masked_score)
    new_peak = jnp.maximum(row_peak, jnp.max(logits, axis=-1))
    rescale = jnp.exp(row_peak - new_peak)
    unnormed = jnp.where(visible, jnp.exp(logits - new_peak[..., None]), 0.0)
    row_total = row_total * rescale + jnp.sum(unnormed, axis=-1)
    weighted = weighted * rescale[..., None] + jnp.einsum(
        "qk,kd->qd", unnormed.astype(jnp.bfloat16), val_heads, preferred_element_type=jnp.float32
    )
    return (new_peak, row_total, weighted)


def per_device(
    query_proj,
    key_proj,
    value_proj,
    hidden,
    out_weight,
    norm_gain,
    segment_ids,
    pad_mask,
    page_table,
):
    tok_count = query_proj.shape[0]
    feat_count = query_proj.shape[1]
    head_count = feat_count // HEAD_DIM
    lo_count = lax.axis_size("seq_lo")
    hi_count = lax.axis_size("seq_hi")
    seq_axes = ("seq_hi", "seq_lo")
    seg_count = lo_count * hi_count // 2
    device_row = lax.axis_index("seq_hi") * lo_count + lax.axis_index("seq_lo")
    tok_index = device_row * tok_count + jnp.arange(tok_count, dtype=jnp.int32)
    member = segment_ids[:, None] == jnp.arange(seg_count, dtype=jnp.int32)[None, :]
    local_first = jnp.min(jnp.where(member, tok_index[:, None], far_index), axis=0)
    first_tok = lax.pmin(local_first, seq_axes)
    position = tok_index - jnp.sum(jnp.where(member, first_tok[None, :], 0), axis=1)
    q_rot = rotate(query_proj, position, head_count, HEAD_DIM)
    k_rot = rotate(key_proj, position, head_count, HEAD_DIM)
    query_tag = segment_ids + 1
    key_tag = jnp.where(pad_mask == 1, segment_ids + 1, 0)

    tags = jnp.stack([key_tag, query_tag], axis=-1).astype(jnp.bfloat16)
    payload = jnp.concatenate(
        [
            q_rot.reshape(tok_count, head_count, HEAD_DIM),
            k_rot.reshape(tok_count, head_count, HEAD_DIM),
            value_proj.reshape(tok_count, head_count, HEAD_DIM),
            jnp.broadcast_to(tags[:, None, :], (tok_count, head_count, 2)),
        ],
        axis=-1,
    ).transpose(1, 0, 2)
    chunk = lax.all_to_all(payload, "seq_lo", 0, 0, tiled=True)
    chunk_count = lo_count * tok_count
    chunk = chunk.reshape(chunk_count, 3 * HEAD_DIM + 2)
    chunk_q = chunk[:, :HEAD_DIM]
    chunk_k = chunk[:, HEAD_DIM : 2 * HEAD_DIM]
    chunk_v = chunk[:, 2 * HEAD_DIM : 3 * HEAD_DIM]
    chunk_ktag = chunk[:, 3 * HEAD_DIM]
    chunk_qtag = chunk[:, 3 * HEAD_DIM + 1]
    ring_own = chunk[:, HEAD_DIM : 3 * HEAD_DIM + 1]

    offsets = jnp.arange(chunk_count, dtype=jnp.int32)
    own_visible = (chunk_ktag[None, :] == chunk_qtag[:, None]) & (
        offsets[None, :] <= offsets[:, None]
    ) | (offsets[None, :] == offsets[:, None])
    softmax_state = (
        jnp.full((chunk_count,), masked_score, jnp.float32),
        jnp.zeros((chunk_count,), jnp.float32),
        jnp.zeros((chunk_count, HEAD_DIM), jnp.float32),
    )
    softmax_state = attend(softmax_state, chunk_q, chunk_k, chunk_v, own_visible)

    def visit_block(current, moved):
        visible = moved[:, 2 * HEAD_DIM][None, :] == chunk_qtag[:, None]
        return attend(
            current, chunk_q, moved[:, :HEAD_DIM], moved[:, HEAD_DIM : 2 * HEAD_DIM], visible
        )

    def cycle_turn(turn_index, loop_state):
        current, moved = loop_state
        following = passed_along(moved, "seq_hi", 1)
        return (visit_block(current, moved), following)

    reach_count = lo_count * hi_count // 2 * tok_count // chunk_count
    moved = passed_along(ring_own, "seq_hi", 1)
    softmax_state, moved = lax.fori_loop(0, reach_count - 1, cycle_turn, (softmax_state, moved))
    softmax_state = visit_block(softmax_state, moved)
    row_peak, row_total, weighted = softmax_state
    chunk_attn = (weighted / row_total[:, None]).astype(jnp.bfloat16)
    back = lax.all_to_all(
        chunk_attn.reshape(lo_count, tok_count, HEAD_DIM), "seq_lo", 0, 0, tiled=True
    )
    attn = back.transpose(1, 0, 2).reshape(tok_count, feat_count)
    partial_value = jnp.dot(attn, out_weight, preferred_element_type=jnp.float32)
    feature_width = hidden.shape[1]
    tp_count = lax.axis_size("tp")
    pieces = (
        partial_value.astype(jnp.bfloat16)
        .reshape(tok_count, tp_count, feature_width)
        .transpose(1, 0, 2)
    )
    gathered = lax.all_to_all(pieces, "tp", 0, 0, tiled=True)
    own_sum = jnp.sum(gathered.astype(jnp.float32), axis=0)
    hidden_out = (hidden.astype(jnp.float32) + own_sum).astype(jnp.bfloat16)
    stream_wide = hidden_out.astype(jnp.float32)
    square_total = lax.psum(jnp.sum(stream_wide * stream_wide, axis=1), "tp")
    normed = (
        stream_wide
        * lax.rsqrt(square_total / D + norm_epsilon)[:, None]
        * norm_gain.astype(jnp.float32)[None, :]
    ).astype(jnp.bfloat16)
    pad_scale = pad_mask.astype(jnp.bfloat16)[:, None]
    page_count = tok_count // PAGE
    stacked = jnp.stack([k_rot * pad_scale, value_proj * pad_scale])
    stacked = stacked.reshape(2, page_count, PAGE, feat_count).transpose(1, 0, 2, 3)
    kv_pages = jnp.zeros_like(stacked).at[page_table].set(stacked)
    return (hidden_out, normed, kv_pages)


def solution(mesh):
    seq_count = mesh.shape["seq"]
    head_count = D // mesh.shape["tp"] // HEAD_DIM
    grouped = Mesh(
        mesh.devices.reshape(seq_count // head_count, head_count, mesh.shape["tp"]),
        ("seq_hi", "seq_lo", "tp"),
    )
    rows = ("seq_hi", "seq_lo")
    placed = (
        P(rows, "tp"),
        P(rows, "tp"),
        P(rows, "tp"),
        P(rows, "tp"),
        P("tp", None),
        P("tp"),
        P(rows),
        P(rows),
        P(rows),
    )
    return jax.shard_map(
        per_device,
        mesh=grouped,
        in_specs=placed,
        out_specs=(P(rows, "tp"), P(rows, "tp"), P(rows, None, None, "tp")),
        check_vma=False,
    )
```

```python
import math

import jax
import jax.numpy as jnp
from jax import lax
from jax.sharding import Mesh, PartitionSpec as P

D = 3072
HEAD_DIM = 96
PAGE = 128


far_index = 1073741824
masked_score = -1e30
norm_epsilon = 1e-05


def passed_along(block, axis, distance):
    devices = range(lax.axis_size(axis))
    route = [(i - distance, i) for i in devices if i - distance in devices]
    return lax.ppermute(block, axis, route)


def rotate(values_in, position, head_count, head_dim):
    count_rows = values_in.shape[0]
    half_dim = head_dim // 2
    frequency = jnp.exp(
        jnp.arange(half_dim, dtype=jnp.float32) * (-2.0 * math.log(10000.0) / head_dim)
    )
    angles = position.astype(jnp.float32)[:, None] * frequency[None, :]
    cosine = jnp.cos(angles)[:, None, :]
    sine_part = jnp.sin(angles)[:, None, :]
    as_float = values_in.astype(jnp.float32).reshape(count_rows, head_count, head_dim)
    lower_half = as_float[..., :half_dim]
    upper_half = as_float[..., half_dim:]
    rotated = jnp.concatenate(
        [
            lower_half * cosine - upper_half * sine_part,
            upper_half * cosine + lower_half * sine_part,
        ],
        axis=-1,
    )
    return rotated.reshape(count_rows, head_count * head_dim).astype(jnp.bfloat16)


def attend(softmax_state, query_heads, key_heads, val_heads, visible):
    row_peak, row_total, weighted = softmax_state
    factor = 1.0 / math.sqrt(HEAD_DIM)
    logits = (
        jnp.einsum("qd,kd->qk", query_heads, key_heads, preferred_element_type=jnp.float32)
        * factor
    )
    logits = jnp.where(visible, logits, masked_score)
    new_peak = jnp.maximum(row_peak, jnp.max(logits, axis=-1))
    rescale = jnp.exp(row_peak - new_peak)
    unnormed = jnp.where(visible, jnp.exp(logits - new_peak[..., None]), 0.0)
    row_total = row_total * rescale + jnp.sum(unnormed, axis=-1)
    weighted = weighted * rescale[..., None] + jnp.einsum(
        "qk,kd->qd", unnormed.astype(jnp.bfloat16), val_heads, preferred_element_type=jnp.float32
    )
    return (new_peak, row_total, weighted)


def per_device(
    query_proj,
    key_proj,
    value_proj,
    hidden,
    out_weight,
    norm_gain,
    segment_ids,
    pad_mask,
    page_table,
):
    tok_count = query_proj.shape[0]
    feat_count = query_proj.shape[1]
    head_count = feat_count // HEAD_DIM
    lo_count = lax.axis_size("seq_lo")
    hi_count = lax.axis_size("seq_hi")
    seg_count = lo_count * hi_count // 2
    device_row = lax.axis_index("seq_hi") * lo_count + lax.axis_index("seq_lo")
    tok_index = device_row * tok_count + jnp.arange(tok_count, dtype=jnp.int32)
    q_rot = rotate(query_proj, tok_index, head_count, HEAD_DIM)
    k_abs = rotate(key_proj, tok_index, head_count, HEAD_DIM)
    query_tag = segment_ids + 1
    key_tag = jnp.where(pad_mask == 1, segment_ids + 1, 0)
    seg_tags = jnp.arange(1, seg_count + 1, dtype=jnp.int32)

    def first_of(tag_values, index_values):
        hit = tag_values[:, None] == seg_tags[None, :].astype(tag_values.dtype)
        return jnp.min(jnp.where(hit, index_values[:, None], far_index), axis=0)

    tags = jnp.stack([key_tag, query_tag], axis=-1).astype(jnp.bfloat16)
    payload = jnp.concatenate(
        [
            q_rot.reshape(tok_count, head_count, HEAD_DIM),
            k_abs.reshape(tok_count, head_count, HEAD_DIM),
            value_proj.reshape(tok_count, head_count, HEAD_DIM),
            jnp.broadcast_to(tags[:, None, :], (tok_count, head_count, 2)),
        ],
        axis=-1,
    ).transpose(1, 0, 2)
    chunk = lax.all_to_all(payload, "seq_lo", 0, 0, tiled=True)
    chunk_count = lo_count * tok_count
    chunk = chunk.reshape(chunk_count, 3 * HEAD_DIM + 2)
    chunk_q = chunk[:, :HEAD_DIM]
    chunk_k = chunk[:, HEAD_DIM : 2 * HEAD_DIM]
    chunk_v = chunk[:, 2 * HEAD_DIM : 3 * HEAD_DIM]
    chunk_ktag = chunk[:, 3 * HEAD_DIM]
    chunk_qtag = chunk[:, 3 * HEAD_DIM + 1]
    ring_own = chunk[:, HEAD_DIM : 3 * HEAD_DIM + 2]
    chunk_row = lax.axis_index("seq_hi")
    chunk_offsets = jnp.arange(chunk_count, dtype=jnp.int32)

    offsets = jnp.arange(chunk_count, dtype=jnp.int32)
    own_visible = (chunk_ktag[None, :] == chunk_qtag[:, None]) & (
        offsets[None, :] <= offsets[:, None]
    ) | (offsets[None, :] == offsets[:, None])
    softmax_state = (
        jnp.full((chunk_count,), masked_score, jnp.float32),
        jnp.zeros((chunk_count,), jnp.float32),
        jnp.zeros((chunk_count, HEAD_DIM), jnp.float32),
    )
    softmax_state = attend(softmax_state, chunk_q, chunk_k, chunk_v, own_visible)

    def visit_block(current, moved, distance):
        state, seen_first = current
        visible = moved[:, 2 * HEAD_DIM][None, :] == chunk_qtag[:, None]
        state = attend(
            state, chunk_q, moved[:, :HEAD_DIM], moved[:, HEAD_DIM : 2 * HEAD_DIM], visible
        )
        moved_index = (chunk_row - distance) * chunk_count + chunk_offsets
        seen_first = jnp.minimum(seen_first, first_of(moved[:, 2 * HEAD_DIM + 1], moved_index))
        return (state, seen_first)

    def cycle_turn(turn_index, loop_state):
        current, moved = loop_state
        following = passed_along(moved, "seq_hi", 1)
        return (visit_block(current, moved, turn_index + 1), following)

    reach_count = lo_count * hi_count // 2 * tok_count // chunk_count
    seen_first = first_of(chunk_qtag, chunk_row * chunk_count + chunk_offsets)
    moved = passed_along(ring_own, "seq_hi", 1)
    (softmax_state, seen_first), moved = lax.fori_loop(
        0, reach_count - 1, cycle_turn, ((softmax_state, seen_first), moved)
    )
    softmax_state, first_tok = visit_block((softmax_state, seen_first), moved, reach_count)
    member = segment_ids[:, None] == jnp.arange(seg_count, dtype=jnp.int32)[None, :]
    position = tok_index - jnp.sum(jnp.where(member, first_tok[None, :], 0), axis=1)
    k_rot = rotate(key_proj, position, head_count, HEAD_DIM)
    row_peak, row_total, weighted = softmax_state
    chunk_attn = (weighted / row_total[:, None]).astype(jnp.bfloat16)
    back = lax.all_to_all(
        chunk_attn.reshape(lo_count, tok_count, HEAD_DIM), "seq_lo", 0, 0, tiled=True
    )
    attn = back.transpose(1, 0, 2).reshape(tok_count, feat_count)
    partial_value = jnp.dot(attn, out_weight, preferred_element_type=jnp.float32)
    feature_width = hidden.shape[1]
    tp_count = lax.axis_size("tp")
    pieces = (
        partial_value.astype(jnp.bfloat16)
        .reshape(tok_count, tp_count, feature_width)
        .transpose(1, 0, 2)
    )
    gathered = lax.all_to_all(pieces, "tp", 0, 0, tiled=True)
    own_sum = jnp.sum(gathered.astype(jnp.float32), axis=0)
    hidden_out = (hidden.astype(jnp.float32) + own_sum).astype(jnp.bfloat16)
    stream_wide = hidden_out.astype(jnp.float32)
    square_part = jnp.sum(stream_wide * stream_wide, axis=1)
    square_total = jnp.sum(
        lax.all_to_all(
            jnp.broadcast_to(square_part[None, :], (tp_count, tok_count)), "tp", 0, 0, tiled=True
        ),
        axis=0,
    )
    normed = (
        stream_wide
        * lax.rsqrt(square_total / D + norm_epsilon)[:, None]
        * norm_gain.astype(jnp.float32)[None, :]
    ).astype(jnp.bfloat16)
    pad_scale = pad_mask.astype(jnp.bfloat16)[:, None]
    page_count = tok_count // PAGE
    stacked = jnp.stack([k_rot * pad_scale, value_proj * pad_scale])
    stacked = stacked.reshape(2, page_count, PAGE, feat_count).transpose(1, 0, 2, 3)
    kv_pages = jnp.zeros_like(stacked).at[page_table].set(stacked)
    return (hidden_out, normed, kv_pages)


def solution(mesh):
    seq_count = mesh.shape["seq"]
    head_count = D // mesh.shape["tp"] // HEAD_DIM
    grouped = Mesh(
        mesh.devices.reshape(seq_count // head_count, head_count, mesh.shape["tp"]),
        ("seq_hi", "seq_lo", "tp"),
    )
    rows = ("seq_hi", "seq_lo")
    placed = (
        P(rows, "tp"),
        P(rows, "tp"),
        P(rows, "tp"),
        P(rows, "tp"),
        P("tp", None),
        P("tp"),
        P(rows),
        P(rows),
        P(rows),
    )
    return jax.shard_map(
        per_device,
        mesh=grouped,
        in_specs=placed,
        out_specs=(P(rows, "tp"), P(rows, "tp"), P(rows, None, None, "tp")),
        check_vma=False,
    )
```

```python
import math

import jax
import jax.numpy as jnp
from jax import lax
from jax.sharding import Mesh, PartitionSpec as P

D = 3072
HEAD_DIM = 96
PAGE = 128


far_index = 1073741824
masked_score = -1e30
norm_epsilon = 1e-05


def passed_along(block, axis, distance):
    devices = range(lax.axis_size(axis))
    route = [(i - distance, i) for i in devices if i - distance in devices]
    return lax.ppermute(block, axis, route)


def rotate(values_in, position, head_count, head_dim):
    count_rows = values_in.shape[0]
    half_dim = head_dim // 2
    frequency = jnp.exp(
        jnp.arange(half_dim, dtype=jnp.float32) * (-2.0 * math.log(10000.0) / head_dim)
    )
    angles = position.astype(jnp.float32)[:, None] * frequency[None, :]
    cosine = jnp.cos(angles)[:, None, :]
    sine_part = jnp.sin(angles)[:, None, :]
    as_float = values_in.astype(jnp.float32).reshape(count_rows, head_count, head_dim)
    lower_half = as_float[..., :half_dim]
    upper_half = as_float[..., half_dim:]
    rotated = jnp.concatenate(
        [
            lower_half * cosine - upper_half * sine_part,
            upper_half * cosine + lower_half * sine_part,
        ],
        axis=-1,
    )
    return rotated.reshape(count_rows, head_count * head_dim).astype(jnp.bfloat16)


def attend(softmax_state, query_heads, key_heads, val_heads, visible):
    row_peak, row_total, weighted = softmax_state
    factor = 1.0 / math.sqrt(HEAD_DIM)
    logits = (
        jnp.einsum("qd,kd->qk", query_heads, key_heads, preferred_element_type=jnp.float32)
        * factor
    )
    logits = jnp.where(visible, logits, masked_score)
    new_peak = jnp.maximum(row_peak, jnp.max(logits, axis=-1))
    rescale = jnp.exp(row_peak - new_peak)
    unnormed = jnp.where(visible, jnp.exp(logits - new_peak[..., None]), 0.0)
    row_total = row_total * rescale + jnp.sum(unnormed, axis=-1)
    weighted = weighted * rescale[..., None] + jnp.einsum(
        "qk,kd->qd", unnormed.astype(jnp.bfloat16), val_heads, preferred_element_type=jnp.float32
    )
    return (new_peak, row_total, weighted)


def per_device(
    query_proj,
    key_proj,
    value_proj,
    hidden,
    out_weight,
    norm_gain,
    segment_ids,
    pad_mask,
    page_table,
):
    tok_count = query_proj.shape[0]
    feat_count = query_proj.shape[1]
    head_count = feat_count // HEAD_DIM
    lo_count = lax.axis_size("seq_lo")
    hi_count = lax.axis_size("seq_hi")
    seg_count = lo_count * hi_count // 2
    device_row = lax.axis_index("seq_hi") * lo_count + lax.axis_index("seq_lo")
    tok_index = device_row * tok_count + jnp.arange(tok_count, dtype=jnp.int32)
    q_rot = rotate(query_proj, tok_index, head_count, HEAD_DIM)
    k_abs = rotate(key_proj, tok_index, head_count, HEAD_DIM)
    query_tag = segment_ids + 1
    key_tag = jnp.where(pad_mask == 1, segment_ids + 1, 0)
    seg_tags = jnp.arange(1, seg_count + 1, dtype=jnp.int32)

    def first_of(tag_values, index_values):
        hit = tag_values[:, None] == seg_tags[None, :].astype(tag_values.dtype)
        return jnp.min(jnp.where(hit, index_values[:, None], far_index), axis=0)

    signed_tag = jnp.where(pad_mask == 1, query_tag, -query_tag)
    all_tags = lax.all_gather(signed_tag, ("seq_hi", "seq_lo"), tiled=True)

    tags = jnp.stack([key_tag, query_tag], axis=-1).astype(jnp.bfloat16)
    payload = jnp.concatenate(
        [
            q_rot.reshape(tok_count, head_count, HEAD_DIM),
            k_abs.reshape(tok_count, head_count, HEAD_DIM),
            value_proj.reshape(tok_count, head_count, HEAD_DIM),
            jnp.broadcast_to(tags[:, None, :], (tok_count, head_count, 2)),
        ],
        axis=-1,
    ).transpose(1, 0, 2)
    chunk = lax.all_to_all(payload, "seq_lo", 0, 0, tiled=True)
    chunk_count = lo_count * tok_count
    chunk = chunk.reshape(chunk_count, 3 * HEAD_DIM + 2)
    chunk_q = chunk[:, :HEAD_DIM]
    chunk_k = chunk[:, HEAD_DIM : 2 * HEAD_DIM]
    chunk_v = chunk[:, 2 * HEAD_DIM : 3 * HEAD_DIM]
    chunk_ktag = chunk[:, 3 * HEAD_DIM]
    chunk_qtag = chunk[:, 3 * HEAD_DIM + 1]
    ring_own = chunk[:, HEAD_DIM : 3 * HEAD_DIM]
    chunk_row = lax.axis_index("seq_hi")
    chunk_offsets = jnp.arange(chunk_count, dtype=jnp.int32)

    offsets = jnp.arange(chunk_count, dtype=jnp.int32)
    own_visible = (chunk_ktag[None, :] == chunk_qtag[:, None]) & (
        offsets[None, :] <= offsets[:, None]
    ) | (offsets[None, :] == offsets[:, None])
    softmax_state = (
        jnp.full((chunk_count,), masked_score, jnp.float32),
        jnp.zeros((chunk_count,), jnp.float32),
        jnp.zeros((chunk_count, HEAD_DIM), jnp.float32),
    )
    softmax_state = attend(softmax_state, chunk_q, chunk_k, chunk_v, own_visible)

    def visit_block(current, moved, distance):
        source_row = chunk_row - distance
        moved_tags = lax.dynamic_slice_in_dim(
            all_tags, jnp.maximum(source_row, 0) * chunk_count, chunk_count
        )
        moved_tags = jnp.where(source_row >= 0, moved_tags, 0).astype(jnp.bfloat16)
        visible = moved_tags[None, :] == chunk_qtag[:, None]
        return attend(
            current, chunk_q, moved[:, :HEAD_DIM], moved[:, HEAD_DIM : 2 * HEAD_DIM], visible
        )

    def cycle_turn(turn_index, loop_state):
        current, moved = loop_state
        following = passed_along(moved, "seq_hi", 1)
        return (visit_block(current, moved, turn_index + 1), following)

    reach_count = lo_count * hi_count // 2 * tok_count // chunk_count
    moved = passed_along(ring_own, "seq_hi", 1)
    softmax_state, moved = lax.fori_loop(0, reach_count - 1, cycle_turn, (softmax_state, moved))
    softmax_state = visit_block(softmax_state, moved, reach_count)
    first_tok = first_of(
        jnp.abs(all_tags), jnp.arange(hi_count * chunk_count, dtype=jnp.int32)
    )
    member = segment_ids[:, None] == jnp.arange(seg_count, dtype=jnp.int32)[None, :]
    position = tok_index - jnp.sum(jnp.where(member, first_tok[None, :], 0), axis=1)
    k_rot = rotate(key_proj, position, head_count, HEAD_DIM)
    row_peak, row_total, weighted = softmax_state
    chunk_attn = (weighted / row_total[:, None]).astype(jnp.bfloat16)
    back = lax.all_to_all(
        chunk_attn.reshape(lo_count, tok_count, HEAD_DIM), "seq_lo", 0, 0, tiled=True
    )
    attn = back.transpose(1, 0, 2).reshape(tok_count, feat_count)
    partial_value = jnp.dot(attn, out_weight, preferred_element_type=jnp.float32)
    feature_width = hidden.shape[1]
    tp_count = lax.axis_size("tp")
    pieces = (
        partial_value.astype(jnp.bfloat16)
        .reshape(tok_count, tp_count, feature_width)
        .transpose(1, 0, 2)
    )
    gathered = lax.all_to_all(pieces, "tp", 0, 0, tiled=True)
    own_sum = jnp.sum(gathered.astype(jnp.float32), axis=0)
    hidden_out = (hidden.astype(jnp.float32) + own_sum).astype(jnp.bfloat16)
    stream_wide = hidden_out.astype(jnp.float32)
    square_part = jnp.sum(stream_wide * stream_wide, axis=1)
    square_total = jnp.sum(
        lax.all_to_all(
            jnp.broadcast_to(square_part[None, :], (tp_count, tok_count)), "tp", 0, 0, tiled=True
        ),
        axis=0,
    )
    normed = (
        stream_wide
        * lax.rsqrt(square_total / D + norm_epsilon)[:, None]
        * norm_gain.astype(jnp.float32)[None, :]
    ).astype(jnp.bfloat16)
    pad_scale = pad_mask.astype(jnp.bfloat16)[:, None]
    page_count = tok_count // PAGE
    stacked = jnp.stack([k_rot * pad_scale, value_proj * pad_scale])
    stacked = stacked.reshape(2, page_count, PAGE, feat_count).transpose(1, 0, 2, 3)
    kv_pages = jnp.zeros_like(stacked).at[page_table].set(stacked)
    return (hidden_out, normed, kv_pages)


def solution(mesh):
    seq_count = mesh.shape["seq"]
    head_count = D // mesh.shape["tp"] // HEAD_DIM
    grouped = Mesh(
        mesh.devices.reshape(seq_count // head_count, head_count, mesh.shape["tp"]),
        ("seq_hi", "seq_lo", "tp"),
    )
    rows = ("seq_hi", "seq_lo")
    placed = (
        P(rows, "tp"),
        P(rows, "tp"),
        P(rows, "tp"),
        P(rows, "tp"),
        P("tp", None),
        P("tp"),
        P(rows),
        P(rows),
        P(rows),
    )
    return jax.shard_map(
        per_device,
        mesh=grouped,
        in_specs=placed,
        out_specs=(P(rows, "tp"), P(rows, "tp"), P(rows, None, None, "tp")),
        check_vma=False,
    )
```

```python
import math

import jax
import jax.numpy as jnp
from jax import lax
from jax.sharding import Mesh, PartitionSpec as P

D = 3072
HEAD_DIM = 96
PAGE = 128


far_index = 1073741824
masked_score = -1e30
norm_epsilon = 1e-05


def passed_along(block, axis, distance):
    devices = range(lax.axis_size(axis))
    route = [(i - distance, i) for i in devices if i - distance in devices]
    return lax.ppermute(block, axis, route)


def rotate(values_in, position, head_count, head_dim):
    count_rows = values_in.shape[0]
    half_dim = head_dim // 2
    frequency = jnp.exp(
        jnp.arange(half_dim, dtype=jnp.float32) * (-2.0 * math.log(10000.0) / head_dim)
    )
    angles = position.astype(jnp.float32)[:, None] * frequency[None, :]
    cosine = jnp.cos(angles)[:, None, :]
    sine_part = jnp.sin(angles)[:, None, :]
    as_float = values_in.astype(jnp.float32).reshape(count_rows, head_count, head_dim)
    lower_half = as_float[..., :half_dim]
    upper_half = as_float[..., half_dim:]
    rotated = jnp.concatenate(
        [
            lower_half * cosine - upper_half * sine_part,
            upper_half * cosine + lower_half * sine_part,
        ],
        axis=-1,
    )
    return rotated.reshape(count_rows, head_count * head_dim).astype(jnp.bfloat16)


def attend(softmax_state, query_heads, key_heads, val_heads, visible):
    row_peak, row_total, weighted = softmax_state
    factor = 1.0 / math.sqrt(HEAD_DIM)
    logits = (
        jnp.einsum("qd,kd->qk", query_heads, key_heads, preferred_element_type=jnp.float32)
        * factor
    )
    logits = jnp.where(visible, logits, masked_score)
    new_peak = jnp.maximum(row_peak, jnp.max(logits, axis=-1))
    rescale = jnp.exp(row_peak - new_peak)
    unnormed = jnp.where(visible, jnp.exp(logits - new_peak[..., None]), 0.0)
    row_total = row_total * rescale + jnp.sum(unnormed, axis=-1)
    weighted = weighted * rescale[..., None] + jnp.einsum(
        "qk,kd->qd", unnormed.astype(jnp.bfloat16), val_heads, preferred_element_type=jnp.float32
    )
    return (new_peak, row_total, weighted)


def per_device(
    query_proj,
    key_proj,
    value_proj,
    hidden,
    out_weight,
    norm_gain,
    segment_ids,
    pad_mask,
    page_table,
):
    tok_count = query_proj.shape[0]
    feat_count = query_proj.shape[1]
    head_count = feat_count // HEAD_DIM
    lo_count = lax.axis_size("seq_lo")
    hi_count = lax.axis_size("seq_hi")
    seg_count = lo_count * hi_count // 2
    device_row = lax.axis_index("seq_hi") * lo_count + lax.axis_index("seq_lo")
    tok_index = device_row * tok_count + jnp.arange(tok_count, dtype=jnp.int32)
    q_rot = rotate(query_proj, tok_index, head_count, HEAD_DIM)
    k_abs = rotate(key_proj, tok_index, head_count, HEAD_DIM)
    query_tag = segment_ids + 1
    key_tag = jnp.where(pad_mask == 1, segment_ids + 1, 0)
    seg_tags = jnp.arange(1, seg_count + 1, dtype=jnp.int32)

    def first_of(tag_values, index_values):
        hit = tag_values[:, None] == seg_tags[None, :].astype(tag_values.dtype)
        return jnp.min(jnp.where(hit, index_values[:, None], far_index), axis=0)

    tags = jnp.stack([key_tag, query_tag], axis=-1).astype(jnp.bfloat16)
    payload = jnp.concatenate(
        [
            q_rot.reshape(tok_count, head_count, HEAD_DIM),
            k_abs.reshape(tok_count, head_count, HEAD_DIM),
            value_proj.reshape(tok_count, head_count, HEAD_DIM),
            jnp.broadcast_to(tags[:, None, :], (tok_count, head_count, 2)),
        ],
        axis=-1,
    ).transpose(1, 0, 2)
    chunk = lax.all_to_all(payload, "seq_lo", 0, 0, tiled=True)
    chunk_count = lo_count * tok_count
    chunk = chunk.reshape(chunk_count, 3 * HEAD_DIM + 2)
    chunk_q = chunk[:, :HEAD_DIM]
    chunk_k = chunk[:, HEAD_DIM : 2 * HEAD_DIM]
    chunk_v = chunk[:, 2 * HEAD_DIM : 3 * HEAD_DIM]
    chunk_ktag = chunk[:, 3 * HEAD_DIM]
    chunk_qtag = chunk[:, 3 * HEAD_DIM + 1]
    signed_tag = jnp.where(chunk_ktag > 0, chunk_qtag, -chunk_qtag)
    ring_own = (chunk[:, HEAD_DIM : 3 * HEAD_DIM], signed_tag.reshape(-1, 128))
    chunk_row = lax.axis_index("seq_hi")
    chunk_offsets = jnp.arange(chunk_count, dtype=jnp.int32)

    offsets = jnp.arange(chunk_count, dtype=jnp.int32)
    own_visible = (chunk_ktag[None, :] == chunk_qtag[:, None]) & (
        offsets[None, :] <= offsets[:, None]
    ) | (offsets[None, :] == offsets[:, None])
    softmax_state = (
        jnp.full((chunk_count,), masked_score, jnp.float32),
        jnp.zeros((chunk_count,), jnp.float32),
        jnp.zeros((chunk_count, HEAD_DIM), jnp.float32),
    )
    softmax_state = attend(softmax_state, chunk_q, chunk_k, chunk_v, own_visible)

    def visit_block(current, moved, distance):
        state, seen_first = current
        moved_kv, moved_tags = moved
        moved_tags = moved_tags.reshape(-1)
        visible = moved_tags[None, :] == chunk_qtag[:, None]
        state = attend(
            state, chunk_q, moved_kv[:, :HEAD_DIM], moved_kv[:, HEAD_DIM:], visible
        )
        moved_index = (chunk_row - distance) * chunk_count + chunk_offsets
        seen_first = jnp.minimum(seen_first, first_of(jnp.abs(moved_tags), moved_index))
        return (state, seen_first)

    def cycle_turn(turn_index, loop_state):
        current, moved = loop_state
        following = passed_along(moved, "seq_hi", 1)
        return (visit_block(current, moved, turn_index + 1), following)

    reach_count = lo_count * hi_count // 2 * tok_count // chunk_count
    seen_first = first_of(chunk_qtag, chunk_row * chunk_count + chunk_offsets)
    moved = passed_along(ring_own, "seq_hi", 1)
    (softmax_state, seen_first), moved = lax.fori_loop(
        0, reach_count - 1, cycle_turn, ((softmax_state, seen_first), moved)
    )
    softmax_state, first_tok = visit_block((softmax_state, seen_first), moved, reach_count)
    member = segment_ids[:, None] == jnp.arange(seg_count, dtype=jnp.int32)[None, :]
    position = tok_index - jnp.sum(jnp.where(member, first_tok[None, :], 0), axis=1)
    k_rot = rotate(key_proj, position, head_count, HEAD_DIM)
    row_peak, row_total, weighted = softmax_state
    chunk_attn = (weighted / row_total[:, None]).astype(jnp.bfloat16)
    back = lax.all_to_all(
        chunk_attn.reshape(lo_count, tok_count, HEAD_DIM), "seq_lo", 0, 0, tiled=True
    )
    attn = back.transpose(1, 0, 2).reshape(tok_count, feat_count)
    partial_value = jnp.dot(attn, out_weight, preferred_element_type=jnp.float32)
    feature_width = hidden.shape[1]
    tp_count = lax.axis_size("tp")
    pieces = (
        partial_value.astype(jnp.bfloat16)
        .reshape(tok_count, tp_count, feature_width)
        .transpose(1, 0, 2)
    )
    gathered = lax.all_to_all(pieces, "tp", 0, 0, tiled=True)
    own_sum = jnp.sum(gathered.astype(jnp.float32), axis=0)
    hidden_out = (hidden.astype(jnp.float32) + own_sum).astype(jnp.bfloat16)
    stream_wide = hidden_out.astype(jnp.float32)
    square_part = jnp.sum(stream_wide * stream_wide, axis=1)
    square_total = jnp.sum(
        lax.all_to_all(
            jnp.broadcast_to(square_part[None, :], (tp_count, tok_count)), "tp", 0, 0, tiled=True
        ),
        axis=0,
    )
    normed = (
        stream_wide
        * lax.rsqrt(square_total / D + norm_epsilon)[:, None]
        * norm_gain.astype(jnp.float32)[None, :]
    ).astype(jnp.bfloat16)
    pad_scale = pad_mask.astype(jnp.bfloat16)[:, None]
    page_count = tok_count // PAGE
    stacked = jnp.stack([k_rot * pad_scale, value_proj * pad_scale])
    stacked = stacked.reshape(2, page_count, PAGE, feat_count).transpose(1, 0, 2, 3)
    kv_pages = jnp.zeros_like(stacked).at[page_table].set(stacked)
    return (hidden_out, normed, kv_pages)


def solution(mesh):
    seq_count = mesh.shape["seq"]
    head_count = D // mesh.shape["tp"] // HEAD_DIM
    grouped = Mesh(
        mesh.devices.reshape(seq_count // head_count, head_count, mesh.shape["tp"]),
        ("seq_hi", "seq_lo", "tp"),
    )
    rows = ("seq_hi", "seq_lo")
    placed = (
        P(rows, "tp"),
        P(rows, "tp"),
        P(rows, "tp"),
        P(rows, "tp"),
        P("tp", None),
        P("tp"),
        P(rows),
        P(rows),
        P(rows),
    )
    return jax.shard_map(
        per_device,
        mesh=grouped,
        in_specs=placed,
        out_specs=(P(rows, "tp"), P(rows, "tp"), P(rows, None, None, "tp")),
        check_vma=False,
    )
```

```python
import math

import jax
import jax.numpy as jnp
from jax import lax
from jax.sharding import Mesh, PartitionSpec as P

D = 3072
HEAD_DIM = 96
PAGE = 128


far_index = 1073741824
masked_score = -1e30
norm_epsilon = 1e-05


def passed_along(block, axis, distance):
    devices = range(lax.axis_size(axis))
    route = [(i - distance, i) for i in devices if i - distance in devices]
    return lax.ppermute(block, axis, route)


def rotate(values_in, position, head_count, head_dim):
    count_rows = values_in.shape[0]
    half_dim = head_dim // 2
    frequency = jnp.exp(
        jnp.arange(half_dim, dtype=jnp.float32) * (-2.0 * math.log(10000.0) / head_dim)
    )
    angles = position.astype(jnp.float32)[:, None] * frequency[None, :]
    cosine = jnp.cos(angles)[:, None, :]
    sine_part = jnp.sin(angles)[:, None, :]
    as_float = values_in.astype(jnp.float32).reshape(count_rows, head_count, head_dim)
    lower_half = as_float[..., :half_dim]
    upper_half = as_float[..., half_dim:]
    rotated = jnp.concatenate(
        [
            lower_half * cosine - upper_half * sine_part,
            upper_half * cosine + lower_half * sine_part,
        ],
        axis=-1,
    )
    return rotated.reshape(count_rows, head_count * head_dim).astype(jnp.bfloat16)


def attend(softmax_state, query_heads, key_heads, val_heads, visible, key_form="kd"):
    row_peak, row_total, weighted = softmax_state
    factor = 1.0 / math.sqrt(HEAD_DIM)
    logits = (
        jnp.einsum(
            "qd," + key_form + "->qk", query_heads, key_heads, preferred_element_type=jnp.float32
        )
        * factor
    )
    logits = jnp.where(visible, logits, masked_score)
    new_peak = jnp.maximum(row_peak, jnp.max(logits, axis=-1))
    rescale = jnp.exp(row_peak - new_peak)
    unnormed = jnp.where(visible, jnp.exp(logits - new_peak[..., None]), 0.0)
    row_total = row_total * rescale + jnp.sum(unnormed, axis=-1)
    weighted = weighted * rescale[..., None] + jnp.einsum(
        "qk," + key_form + "->qd",
        unnormed.astype(jnp.bfloat16),
        val_heads,
        preferred_element_type=jnp.float32,
    )
    return (new_peak, row_total, weighted)


def per_device(
    query_proj,
    key_proj,
    value_proj,
    hidden,
    out_weight,
    norm_gain,
    segment_ids,
    pad_mask,
    page_table,
):
    tok_count = query_proj.shape[0]
    feat_count = query_proj.shape[1]
    head_count = feat_count // HEAD_DIM
    lo_count = lax.axis_size("seq_lo")
    hi_count = lax.axis_size("seq_hi")
    seg_count = lo_count * hi_count // 2
    device_row = lax.axis_index("seq_hi") * lo_count + lax.axis_index("seq_lo")
    tok_index = device_row * tok_count + jnp.arange(tok_count, dtype=jnp.int32)
    q_rot = rotate(query_proj, tok_index, head_count, HEAD_DIM)
    k_abs = rotate(key_proj, tok_index, head_count, HEAD_DIM)
    query_tag = segment_ids + 1
    key_tag = jnp.where(pad_mask == 1, segment_ids + 1, 0)
    seg_tags = jnp.arange(1, seg_count + 1, dtype=jnp.int32)

    def first_of(tag_values, index_values):
        hit = tag_values[:, None] == seg_tags[None, :].astype(tag_values.dtype)
        return jnp.min(jnp.where(hit, index_values[:, None], far_index), axis=0)

    tags = jnp.stack([key_tag, query_tag], axis=-1).astype(jnp.bfloat16)
    payload = jnp.concatenate(
        [
            q_rot.reshape(tok_count, head_count, HEAD_DIM),
            k_abs.reshape(tok_count, head_count, HEAD_DIM),
            value_proj.reshape(tok_count, head_count, HEAD_DIM),
            jnp.broadcast_to(tags[:, None, :], (tok_count, head_count, 2)),
        ],
        axis=-1,
    ).transpose(1, 0, 2)
    chunk = lax.all_to_all(payload, "seq_lo", 0, 0, tiled=True)
    chunk_count = lo_count * tok_count
    chunk = chunk.reshape(chunk_count, 3 * HEAD_DIM + 2)
    chunk_q = chunk[:, :HEAD_DIM]
    chunk_k = chunk[:, HEAD_DIM : 2 * HEAD_DIM]
    chunk_v = chunk[:, 2 * HEAD_DIM : 3 * HEAD_DIM]
    chunk_ktag = chunk[:, 3 * HEAD_DIM]
    chunk_qtag = chunk[:, 3 * HEAD_DIM + 1]
    signed_tag = jnp.where(chunk_ktag > 0, chunk_qtag, -chunk_qtag)
    ring_own = (chunk[:, HEAD_DIM : 3 * HEAD_DIM].T, signed_tag.reshape(-1, 128))
    chunk_row = lax.axis_index("seq_hi")
    chunk_offsets = jnp.arange(chunk_count, dtype=jnp.int32)

    offsets = jnp.arange(chunk_count, dtype=jnp.int32)
    own_visible = (chunk_ktag[None, :] == chunk_qtag[:, None]) & (
        offsets[None, :] <= offsets[:, None]
    ) | (offsets[None, :] == offsets[:, None])
    softmax_state = (
        jnp.full((chunk_count,), masked_score, jnp.float32),
        jnp.zeros((chunk_count,), jnp.float32),
        jnp.zeros((chunk_count, HEAD_DIM), jnp.float32),
    )
    softmax_state = attend(softmax_state, chunk_q, chunk_k, chunk_v, own_visible)

    def visit_block(current, moved, distance):
        state, seen_first = current
        moved_kv, moved_tags = moved
        moved_tags = moved_tags.reshape(-1)
        visible = moved_tags[None, :] == chunk_qtag[:, None]
        state = attend(
            state, chunk_q, moved_kv[:HEAD_DIM], moved_kv[HEAD_DIM:], visible, "dk"
        )
        moved_index = (chunk_row - distance) * chunk_count + chunk_offsets
        seen_first = jnp.minimum(seen_first, first_of(jnp.abs(moved_tags), moved_index))
        return (state, seen_first)

    def cycle_turn(turn_index, loop_state):
        current, moved = loop_state
        following = passed_along(moved, "seq_hi", 1)
        return (visit_block(current, moved, turn_index + 1), following)

    reach_count = lo_count * hi_count // 2 * tok_count // chunk_count
    seen_first = first_of(chunk_qtag, chunk_row * chunk_count + chunk_offsets)
    moved = passed_along(ring_own, "seq_hi", 1)
    (softmax_state, seen_first), moved = lax.fori_loop(
        0, reach_count - 1, cycle_turn, ((softmax_state, seen_first), moved)
    )
    softmax_state, first_tok = visit_block((softmax_state, seen_first), moved, reach_count)
    member = segment_ids[:, None] == jnp.arange(seg_count, dtype=jnp.int32)[None, :]
    position = tok_index - jnp.sum(jnp.where(member, first_tok[None, :], 0), axis=1)
    k_rot = rotate(key_proj, position, head_count, HEAD_DIM)
    row_peak, row_total, weighted = softmax_state
    chunk_attn = (weighted / row_total[:, None]).astype(jnp.bfloat16)
    back = lax.all_to_all(
        chunk_attn.reshape(lo_count, tok_count, HEAD_DIM), "seq_lo", 0, 0, tiled=True
    )
    attn = back.transpose(1, 0, 2).reshape(tok_count, feat_count)
    partial_value = jnp.dot(attn, out_weight, preferred_element_type=jnp.float32)
    feature_width = hidden.shape[1]
    tp_count = lax.axis_size("tp")
    pieces = (
        partial_value.astype(jnp.bfloat16)
        .reshape(tok_count, tp_count, feature_width)
        .transpose(1, 0, 2)
    )
    gathered = lax.all_to_all(pieces, "tp", 0, 0, tiled=True)
    own_sum = jnp.sum(gathered.astype(jnp.float32), axis=0)
    hidden_out = (hidden.astype(jnp.float32) + own_sum).astype(jnp.bfloat16)
    stream_wide = hidden_out.astype(jnp.float32)
    square_part = jnp.sum(stream_wide * stream_wide, axis=1)
    square_total = jnp.sum(
        lax.all_to_all(
            jnp.broadcast_to(square_part[None, :], (tp_count, tok_count)), "tp", 0, 0, tiled=True
        ),
        axis=0,
    )
    normed = (
        stream_wide
        * lax.rsqrt(square_total / D + norm_epsilon)[:, None]
        * norm_gain.astype(jnp.float32)[None, :]
    ).astype(jnp.bfloat16)
    pad_scale = pad_mask.astype(jnp.bfloat16)[:, None]
    page_count = tok_count // PAGE
    stacked = jnp.stack([k_rot * pad_scale, value_proj * pad_scale])
    stacked = stacked.reshape(2, page_count, PAGE, feat_count).transpose(1, 0, 2, 3)
    kv_pages = jnp.zeros_like(stacked).at[page_table].set(stacked)
    return (hidden_out, normed, kv_pages)


def solution(mesh):
    seq_count = mesh.shape["seq"]
    head_count = D // mesh.shape["tp"] // HEAD_DIM
    grouped = Mesh(
        mesh.devices.reshape(seq_count // head_count, head_count, mesh.shape["tp"]),
        ("seq_hi", "seq_lo", "tp"),
    )
    rows = ("seq_hi", "seq_lo")
    placed = (
        P(rows, "tp"),
        P(rows, "tp"),
        P(rows, "tp"),
        P(rows, "tp"),
        P("tp", None),
        P("tp"),
        P(rows),
        P(rows),
        P(rows),
    )
    return jax.shard_map(
        per_device,
        mesh=grouped,
        in_specs=placed,
        out_specs=(P(rows, "tp"), P(rows, "tp"), P(rows, None, None, "tp")),
        check_vma=False,
    )
```

```python
import math

import jax
import jax.numpy as jnp
from jax import lax
from jax.sharding import Mesh, PartitionSpec as P

D = 3072
HEAD_DIM = 96
PAGE = 128


far_index = 1073741824
masked_score = -1e30
norm_epsilon = 1e-05


def passed_along(block, axis, distance):
    devices = range(lax.axis_size(axis))
    route = [(i - distance, i) for i in devices if i - distance in devices]
    return lax.ppermute(block, axis, route)


def rotate(values_in, position, head_count, head_dim):
    count_rows = values_in.shape[0]
    half_dim = head_dim // 2
    frequency = jnp.exp(
        jnp.arange(half_dim, dtype=jnp.float32) * (-2.0 * math.log(10000.0) / head_dim)
    )
    angles = position.astype(jnp.float32)[:, None] * frequency[None, :]
    cosine = jnp.cos(angles)[:, None, :]
    sine_part = jnp.sin(angles)[:, None, :]
    as_float = values_in.astype(jnp.float32).reshape(count_rows, head_count, head_dim)
    lower_half = as_float[..., :half_dim]
    upper_half = as_float[..., half_dim:]
    rotated = jnp.concatenate(
        [
            lower_half * cosine - upper_half * sine_part,
            upper_half * cosine + lower_half * sine_part,
        ],
        axis=-1,
    )
    return rotated.reshape(count_rows, head_count * head_dim).astype(jnp.bfloat16)


def attend(softmax_state, query_heads, key_heads, val_heads, visible):
    row_peak, row_total, weighted = softmax_state
    factor = 1.0 / math.sqrt(HEAD_DIM)
    logits = (
        jnp.einsum("qd,kd->qk", query_heads, key_heads, preferred_element_type=jnp.float32)
        * factor
    )
    logits = jnp.where(visible, logits, masked_score)
    new_peak = jnp.maximum(row_peak, jnp.max(logits, axis=-1))
    rescale = jnp.exp(row_peak - new_peak)
    unnormed = jnp.where(visible, jnp.exp(logits - new_peak[..., None]), 0.0)
    row_total = row_total * rescale + jnp.sum(unnormed, axis=-1)
    weighted = weighted * rescale[..., None] + jnp.einsum(
        "qk,kd->qd", unnormed.astype(jnp.bfloat16), val_heads, preferred_element_type=jnp.float32
    )
    return (new_peak, row_total, weighted)


def per_device(
    query_proj,
    key_proj,
    value_proj,
    hidden,
    out_weight,
    norm_gain,
    segment_ids,
    pad_mask,
    page_table,
):
    tok_count = query_proj.shape[0]
    feat_count = query_proj.shape[1]
    head_count = feat_count // HEAD_DIM
    lo_count = lax.axis_size("seq_lo")
    hi_count = lax.axis_size("seq_hi")
    seg_count = lo_count * hi_count // 2
    device_row = lax.axis_index("seq_hi") * lo_count + lax.axis_index("seq_lo")
    tok_index = device_row * tok_count + jnp.arange(tok_count, dtype=jnp.int32)
    q_rot = rotate(query_proj, tok_index, head_count, HEAD_DIM)
    k_abs = rotate(key_proj, tok_index, head_count, HEAD_DIM)
    query_tag = segment_ids + 1
    key_tag = jnp.where(pad_mask == 1, segment_ids + 1, 0)
    seg_tags = jnp.arange(1, seg_count + 1, dtype=jnp.int32)

    def first_of(tag_values, index_values):
        hit = tag_values[:, None] == seg_tags[None, :].astype(tag_values.dtype)
        return jnp.min(jnp.where(hit, index_values[:, None], far_index), axis=0)

    tags = jnp.stack([key_tag, query_tag], axis=-1).astype(jnp.bfloat16)
    payload = jnp.concatenate(
        [
            q_rot.reshape(tok_count, head_count, HEAD_DIM),
            k_abs.reshape(tok_count, head_count, HEAD_DIM),
            value_proj.reshape(tok_count, head_count, HEAD_DIM),
            jnp.broadcast_to(tags[:, None, :], (tok_count, head_count, 2)),
        ],
        axis=-1,
    ).transpose(1, 0, 2)
    chunk = lax.all_to_all(payload, "seq_lo", 0, 0, tiled=True)
    chunk_count = lo_count * tok_count
    chunk = chunk.reshape(chunk_count, 3 * HEAD_DIM + 2)
    chunk_q = chunk[:, :HEAD_DIM]
    chunk_k = chunk[:, HEAD_DIM : 2 * HEAD_DIM]
    chunk_v = chunk[:, 2 * HEAD_DIM : 3 * HEAD_DIM]
    chunk_ktag = chunk[:, 3 * HEAD_DIM]
    chunk_qtag = chunk[:, 3 * HEAD_DIM + 1]
    ring_own = chunk[:, HEAD_DIM : 3 * HEAD_DIM + 2]
    chunk_row = lax.axis_index("seq_hi")
    chunk_offsets = jnp.arange(chunk_count, dtype=jnp.int32)

    offsets = jnp.arange(chunk_count, dtype=jnp.int32)
    own_visible = (chunk_ktag[None, :] == chunk_qtag[:, None]) & (
        offsets[None, :] <= offsets[:, None]
    ) | (offsets[None, :] == offsets[:, None])
    softmax_state = (
        jnp.full((chunk_count,), masked_score, jnp.float32),
        jnp.zeros((chunk_count,), jnp.float32),
        jnp.zeros((chunk_count, HEAD_DIM), jnp.float32),
    )
    softmax_state = attend(softmax_state, chunk_q, chunk_k, chunk_v, own_visible)

    def visit_block(current, moved, distance):
        state, seen_first = current
        visible = moved[:, 2 * HEAD_DIM][None, :] == chunk_qtag[:, None]
        state = attend(
            state, chunk_q, moved[:, :HEAD_DIM], moved[:, HEAD_DIM : 2 * HEAD_DIM], visible
        )
        moved_index = (chunk_row - distance) * chunk_count + chunk_offsets
        seen_first = jnp.minimum(seen_first, first_of(moved[:, 2 * HEAD_DIM + 1], moved_index))
        return (state, seen_first)

    def cycle_turn(turn_index, loop_state):
        current, moved = loop_state
        following = passed_along(moved, "seq_hi", 1)
        return (visit_block(current, moved, turn_index + 1), following)

    reach_count = lo_count * hi_count // 2 * tok_count // chunk_count
    seen_first = first_of(chunk_qtag, chunk_row * chunk_count + chunk_offsets)
    moved = passed_along(ring_own, "seq_hi", 1)
    loop_state = ((softmax_state, seen_first), moved)
    for turn_index in range(reach_count - 1):
        loop_state = cycle_turn(turn_index, loop_state)
    (softmax_state, seen_first), moved = loop_state
    softmax_state, first_tok = visit_block((softmax_state, seen_first), moved, reach_count)
    member = segment_ids[:, None] == jnp.arange(seg_count, dtype=jnp.int32)[None, :]
    position = tok_index - jnp.sum(jnp.where(member, first_tok[None, :], 0), axis=1)
    k_rot = rotate(key_proj, position, head_count, HEAD_DIM)
    row_peak, row_total, weighted = softmax_state
    chunk_attn = (weighted / row_total[:, None]).astype(jnp.bfloat16)
    back = lax.all_to_all(
        chunk_attn.reshape(lo_count, tok_count, HEAD_DIM), "seq_lo", 0, 0, tiled=True
    )
    attn = back.transpose(1, 0, 2).reshape(tok_count, feat_count)
    partial_value = jnp.dot(attn, out_weight, preferred_element_type=jnp.float32)
    feature_width = hidden.shape[1]
    tp_count = lax.axis_size("tp")
    pieces = (
        partial_value.astype(jnp.bfloat16)
        .reshape(tok_count, tp_count, feature_width)
        .transpose(1, 0, 2)
    )
    gathered = lax.all_to_all(pieces, "tp", 0, 0, tiled=True)
    own_sum = jnp.sum(gathered.astype(jnp.float32), axis=0)
    hidden_out = (hidden.astype(jnp.float32) + own_sum).astype(jnp.bfloat16)
    stream_wide = hidden_out.astype(jnp.float32)
    square_part = jnp.sum(stream_wide * stream_wide, axis=1)
    square_total = jnp.sum(
        lax.all_to_all(
            jnp.broadcast_to(square_part[None, :], (tp_count, tok_count)), "tp", 0, 0, tiled=True
        ),
        axis=0,
    )
    normed = (
        stream_wide
        * lax.rsqrt(square_total / D + norm_epsilon)[:, None]
        * norm_gain.astype(jnp.float32)[None, :]
    ).astype(jnp.bfloat16)
    pad_scale = pad_mask.astype(jnp.bfloat16)[:, None]
    page_count = tok_count // PAGE
    stacked = jnp.stack([k_rot * pad_scale, value_proj * pad_scale])
    stacked = stacked.reshape(2, page_count, PAGE, feat_count).transpose(1, 0, 2, 3)
    kv_pages = jnp.zeros_like(stacked).at[page_table].set(stacked)
    return (hidden_out, normed, kv_pages)


def solution(mesh):
    seq_count = mesh.shape["seq"]
    head_count = D // mesh.shape["tp"] // HEAD_DIM
    grouped = Mesh(
        mesh.devices.reshape(seq_count // head_count, head_count, mesh.shape["tp"]),
        ("seq_hi", "seq_lo", "tp"),
    )
    rows = ("seq_hi", "seq_lo")
    placed = (
        P(rows, "tp"),
        P(rows, "tp"),
        P(rows, "tp"),
        P(rows, "tp"),
        P("tp", None),
        P("tp"),
        P(rows),
        P(rows),
        P(rows),
    )
    return jax.shard_map(
        per_device,
        mesh=grouped,
        in_specs=placed,
        out_specs=(P(rows, "tp"), P(rows, "tp"), P(rows, None, None, "tp")),
        check_vma=False,
    )
```

```python
import math

import jax
import jax.numpy as jnp
from jax import lax
from jax.sharding import Mesh, PartitionSpec as P

D = 3072
HEAD_DIM = 96
PAGE = 128


far_index = 1073741824
masked_score = -1e30
norm_epsilon = 1e-05


def passed_along(block, axis, distance):
    devices = range(lax.axis_size(axis))
    route = [(i - distance, i) for i in devices if i - distance in devices]
    return lax.ppermute(block, axis, route)


def rotate(values_in, position, head_count, head_dim):
    count_rows = values_in.shape[0]
    half_dim = head_dim // 2
    frequency = jnp.exp(
        jnp.arange(half_dim, dtype=jnp.float32) * (-2.0 * math.log(10000.0) / head_dim)
    )
    angles = position.astype(jnp.float32)[:, None] * frequency[None, :]
    cosine = jnp.cos(angles)[:, None, :]
    sine_part = jnp.sin(angles)[:, None, :]
    as_float = values_in.astype(jnp.float32).reshape(count_rows, head_count, head_dim)
    lower_half = as_float[..., :half_dim]
    upper_half = as_float[..., half_dim:]
    rotated = jnp.concatenate(
        [
            lower_half * cosine - upper_half * sine_part,
            upper_half * cosine + lower_half * sine_part,
        ],
        axis=-1,
    )
    return rotated.reshape(count_rows, head_count * head_dim).astype(jnp.bfloat16)


def attend(softmax_state, query_heads, key_heads, val_heads, visible):
    row_peak, row_total, weighted = softmax_state
    factor = 1.0 / math.sqrt(HEAD_DIM)
    logits = (
        jnp.einsum("qd,kd->qk", query_heads, key_heads, preferred_element_type=jnp.float32)
        * factor
    )
    logits = jnp.where(visible, logits, masked_score)
    new_peak = jnp.maximum(row_peak, jnp.max(logits, axis=-1))
    rescale = jnp.exp(row_peak - new_peak)
    unnormed = jnp.where(visible, jnp.exp(logits - new_peak[..., None]), 0.0)
    row_total = row_total * rescale + jnp.sum(unnormed, axis=-1)
    weighted = weighted * rescale[..., None] + jnp.einsum(
        "qk,kd->qd", unnormed.astype(jnp.bfloat16), val_heads, preferred_element_type=jnp.float32
    )
    return (new_peak, row_total, weighted)


def per_device(
    query_proj,
    key_proj,
    value_proj,
    hidden,
    out_weight,
    norm_gain,
    segment_ids,
    pad_mask,
    page_table,
):
    tok_count = query_proj.shape[0]
    feat_count = query_proj.shape[1]
    head_count = feat_count // HEAD_DIM
    lo_count = lax.axis_size("seq_lo")
    hi_count = lax.axis_size("seq_hi")
    seg_count = lo_count * hi_count // 2
    device_row = lax.axis_index("seq_hi") * lo_count + lax.axis_index("seq_lo")
    tok_index = device_row * tok_count + jnp.arange(tok_count, dtype=jnp.int32)
    q_rot = rotate(query_proj, tok_index, head_count, HEAD_DIM)
    k_abs = rotate(key_proj, tok_index, head_count, HEAD_DIM)
    query_tag = segment_ids + 1
    key_tag = jnp.where(pad_mask == 1, segment_ids + 1, 0)
    seg_tags = jnp.arange(1, seg_count + 1, dtype=jnp.int32)

    def first_of(tag_values, index_values):
        hit = tag_values[:, None] == seg_tags[None, :].astype(tag_values.dtype)
        return jnp.min(jnp.where(hit, index_values[:, None], far_index), axis=0)

    tags = jnp.stack([key_tag, query_tag], axis=-1).astype(jnp.bfloat16)
    payload = jnp.concatenate(
        [
            q_rot.reshape(tok_count, head_count, HEAD_DIM),
            k_abs.reshape(tok_count, head_count, HEAD_DIM),
            value_proj.reshape(tok_count, head_count, HEAD_DIM),
            jnp.broadcast_to(tags[:, None, :], (tok_count, head_count, 2)),
        ],
        axis=-1,
    ).transpose(1, 0, 2)
    chunk = lax.all_to_all(payload, "seq_lo", 0, 0, tiled=True)
    chunk_count = lo_count * tok_count
    chunk = chunk.reshape(chunk_count, 3 * HEAD_DIM + 2)
    chunk_q = chunk[:, :HEAD_DIM]
    chunk_k = chunk[:, HEAD_DIM : 2 * HEAD_DIM]
    chunk_v = chunk[:, 2 * HEAD_DIM : 3 * HEAD_DIM]
    chunk_ktag = chunk[:, 3 * HEAD_DIM]
    chunk_qtag = chunk[:, 3 * HEAD_DIM + 1]
    ring_own = chunk[:, HEAD_DIM : 3 * HEAD_DIM + 2]
    chunk_row = lax.axis_index("seq_hi")
    chunk_offsets = jnp.arange(chunk_count, dtype=jnp.int32)

    offsets = jnp.arange(chunk_count, dtype=jnp.int32)
    own_visible = (chunk_ktag[None, :] == chunk_qtag[:, None]) & (
        offsets[None, :] <= offsets[:, None]
    ) | (offsets[None, :] == offsets[:, None])
    softmax_state = (
        jnp.full((chunk_count,), masked_score, jnp.float32),
        jnp.zeros((chunk_count,), jnp.float32),
        jnp.zeros((chunk_count, HEAD_DIM), jnp.float32),
    )
    softmax_state = attend(softmax_state, chunk_q, chunk_k, chunk_v, own_visible)

    def visit_block(current, moved, distance):
        state, seen_first = current
        visible = moved[:, 2 * HEAD_DIM][None, :] == chunk_qtag[:, None]
        state = attend(
            state, chunk_q, moved[:, :HEAD_DIM], moved[:, HEAD_DIM : 2 * HEAD_DIM], visible
        )
        moved_index = (chunk_row - distance) * chunk_count + chunk_offsets
        seen_first = jnp.minimum(seen_first, first_of(moved[:, 2 * HEAD_DIM + 1], moved_index))
        return (state, seen_first)

    def cycle_turn(turn_index, loop_state):
        current, moved = loop_state
        following = passed_along(moved, "seq_hi", 1)
        return (visit_block(current, moved, turn_index + 1), following)

    reach_count = lo_count * hi_count // 2 * tok_count // chunk_count
    seen_first = first_of(chunk_qtag, chunk_row * chunk_count + chunk_offsets)
    moved = passed_along(ring_own, "seq_hi", 1)
    (softmax_state, seen_first), moved = lax.fori_loop(
        0, reach_count - 1, cycle_turn, ((softmax_state, seen_first), moved)
    )
    softmax_state, first_tok = visit_block((softmax_state, seen_first), moved, reach_count)
    member = segment_ids[:, None] == jnp.arange(seg_count, dtype=jnp.int32)[None, :]
    position = tok_index - jnp.sum(jnp.where(member, first_tok[None, :], 0), axis=1)
    k_rot = rotate(key_proj, position, head_count, HEAD_DIM)
    row_peak, row_total, weighted = softmax_state
    chunk_attn = (weighted / row_total[:, None]).astype(jnp.bfloat16)
    back = lax.all_to_all(
        chunk_attn.reshape(lo_count, tok_count, HEAD_DIM), "seq_lo", 0, 0, tiled=True
    )
    attn = back.transpose(1, 0, 2).reshape(tok_count, feat_count)
    partial_value = jnp.dot(attn, out_weight, preferred_element_type=jnp.float32)
    feature_width = hidden.shape[1]
    tp_hi_count = lax.axis_size("tp_hi")
    tp_lo_count = lax.axis_size("tp_lo")
    tp_count = tp_hi_count * tp_lo_count
    pieces = (
        partial_value.astype(jnp.bfloat16)
        .reshape(tok_count, tp_hi_count, tp_lo_count, feature_width)
        .transpose(2, 1, 0, 3)
    )
    near = lax.all_to_all(pieces, "tp_lo", 0, 0, tiled=True)
    near_sum = jnp.sum(near.astype(jnp.float32), axis=0).astype(jnp.bfloat16)
    far = lax.all_to_all(near_sum, "tp_hi", 0, 0, tiled=True)
    own_sum = jnp.sum(far.astype(jnp.float32), axis=0)
    hidden_out = (hidden.astype(jnp.float32) + own_sum).astype(jnp.bfloat16)
    stream_wide = hidden_out.astype(jnp.float32)
    square_part = jnp.sum(stream_wide * stream_wide, axis=1)
    square_total = jnp.sum(
        lax.all_to_all(
            jnp.broadcast_to(square_part[None, :], (tp_count, tok_count)),
            ("tp_hi", "tp_lo"),
            0,
            0,
            tiled=True,
        ),
        axis=0,
    )
    normed = (
        stream_wide
        * lax.rsqrt(square_total / D + norm_epsilon)[:, None]
        * norm_gain.astype(jnp.float32)[None, :]
    ).astype(jnp.bfloat16)
    pad_scale = pad_mask.astype(jnp.bfloat16)[:, None]
    page_count = tok_count // PAGE
    stacked = jnp.stack([k_rot * pad_scale, value_proj * pad_scale])
    stacked = stacked.reshape(2, page_count, PAGE, feat_count).transpose(1, 0, 2, 3)
    kv_pages = jnp.zeros_like(stacked).at[page_table].set(stacked)
    return (hidden_out, normed, kv_pages)


def solution(mesh):
    seq_count = mesh.shape["seq"]
    tp_count = mesh.shape["tp"]
    head_count = D // tp_count // HEAD_DIM
    grouped = Mesh(
        mesh.devices.reshape(seq_count // head_count, head_count, tp_count // 2, 2),
        ("seq_hi", "seq_lo", "tp_hi", "tp_lo"),
    )
    rows = ("seq_hi", "seq_lo")
    cols = ("tp_hi", "tp_lo")
    placed = (
        P(rows, cols),
        P(rows, cols),
        P(rows, cols),
        P(rows, cols),
        P(cols, None),
        P(cols),
        P(rows),
        P(rows),
        P(rows),
    )
    return jax.shard_map(
        per_device,
        mesh=grouped,
        in_specs=placed,
        out_specs=(P(rows, cols), P(rows, cols), P(rows, None, None, cols)),
        check_vma=False,
    )
```

```python
import math

import jax
import jax.numpy as jnp
from jax import lax
from jax.sharding import Mesh, PartitionSpec as P

D = 3072
HEAD_DIM = 96
PAGE = 128


far_index = 1073741824
masked_score = -1e30
norm_epsilon = 1e-05


def passed_along(block, axis, distance):
    devices = range(lax.axis_size(axis))
    route = [(i - distance, i) for i in devices if i - distance in devices]
    return lax.ppermute(block, axis, route)


def rotate(values_in, position, head_count, head_dim):
    count_rows = values_in.shape[0]
    half_dim = head_dim // 2
    frequency = jnp.exp(
        jnp.arange(half_dim, dtype=jnp.float32) * (-2.0 * math.log(10000.0) / head_dim)
    )
    angles = position.astype(jnp.float32)[:, None] * frequency[None, :]
    cosine = jnp.cos(angles)[:, None, :]
    sine_part = jnp.sin(angles)[:, None, :]
    as_float = values_in.astype(jnp.float32).reshape(count_rows, head_count, head_dim)
    lower_half = as_float[..., :half_dim]
    upper_half = as_float[..., half_dim:]
    rotated = jnp.concatenate(
        [
            lower_half * cosine - upper_half * sine_part,
            upper_half * cosine + lower_half * sine_part,
        ],
        axis=-1,
    )
    return rotated.reshape(count_rows, head_count * head_dim).astype(jnp.bfloat16)


def attend(softmax_state, query_heads, key_heads, val_heads, visible):
    row_peak, row_total, weighted = softmax_state
    factor = 1.0 / math.sqrt(HEAD_DIM)
    logits = (
        jnp.einsum("qd,kd->qk", query_heads, key_heads, preferred_element_type=jnp.float32)
        * factor
    )
    logits = jnp.where(visible, logits, masked_score)
    new_peak = jnp.maximum(row_peak, jnp.max(logits, axis=-1))
    rescale = jnp.exp(row_peak - new_peak)
    unnormed = jnp.where(visible, jnp.exp(logits - new_peak[..., None]), 0.0)
    row_total = row_total * rescale + jnp.sum(unnormed, axis=-1)
    weighted = weighted * rescale[..., None] + jnp.einsum(
        "qk,kd->qd", unnormed.astype(jnp.bfloat16), val_heads, preferred_element_type=jnp.float32
    )
    return (new_peak, row_total, weighted)


def per_device(
    query_proj,
    key_proj,
    value_proj,
    hidden,
    out_weight,
    norm_gain,
    segment_ids,
    pad_mask,
    page_table,
):
    tok_count = query_proj.shape[0]
    feat_count = query_proj.shape[1]
    head_count = feat_count // HEAD_DIM
    lo_count = lax.axis_size("seq_lo")
    hi_count = lax.axis_size("seq_hi")
    seg_count = lo_count * hi_count // 2
    device_row = lax.axis_index("seq_hi") * lo_count + lax.axis_index("seq_lo")
    tok_index = device_row * tok_count + jnp.arange(tok_count, dtype=jnp.int32)
    q_rot = rotate(query_proj, tok_index, head_count, HEAD_DIM)
    k_abs = rotate(key_proj, tok_index, head_count, HEAD_DIM)
    query_tag = segment_ids + 1
    key_tag = jnp.where(pad_mask == 1, segment_ids + 1, 0)
    seg_tags = jnp.arange(1, seg_count + 1, dtype=jnp.int32)

    def first_of(tag_values, index_values):
        hit = tag_values[:, None] == seg_tags[None, :].astype(tag_values.dtype)
        return jnp.min(jnp.where(hit, index_values[:, None], far_index), axis=0)

    tags = jnp.stack([key_tag, query_tag], axis=-1).astype(jnp.bfloat16)
    payload = jnp.concatenate(
        [
            q_rot.reshape(tok_count, head_count, HEAD_DIM),
            k_abs.reshape(tok_count, head_count, HEAD_DIM),
            value_proj.reshape(tok_count, head_count, HEAD_DIM),
            jnp.broadcast_to(tags[:, None, :], (tok_count, head_count, 2)),
        ],
        axis=-1,
    ).transpose(1, 0, 2)
    chunk = lax.all_to_all(payload, "seq_lo", 0, 0, tiled=True)
    chunk_count = lo_count * tok_count
    chunk = chunk.reshape(chunk_count, 3 * HEAD_DIM + 2)
    chunk_q = chunk[:, :HEAD_DIM]
    chunk_k = chunk[:, HEAD_DIM : 2 * HEAD_DIM]
    chunk_v = chunk[:, 2 * HEAD_DIM : 3 * HEAD_DIM]
    chunk_ktag = chunk[:, 3 * HEAD_DIM]
    chunk_qtag = chunk[:, 3 * HEAD_DIM + 1]
    ring_own = chunk[:, HEAD_DIM : 3 * HEAD_DIM + 2]
    chunk_row = lax.axis_index("seq_hi")
    chunk_offsets = jnp.arange(chunk_count, dtype=jnp.int32)

    offsets = jnp.arange(chunk_count, dtype=jnp.int32)
    own_visible = (chunk_ktag[None, :] == chunk_qtag[:, None]) & (
        offsets[None, :] <= offsets[:, None]
    ) | (offsets[None, :] == offsets[:, None])
    softmax_state = (
        jnp.full((chunk_count,), masked_score, jnp.float32),
        jnp.zeros((chunk_count,), jnp.float32),
        jnp.zeros((chunk_count, HEAD_DIM), jnp.float32),
    )
    softmax_state = attend(softmax_state, chunk_q, chunk_k, chunk_v, own_visible)

    def visit_block(current, moved, distance):
        state, seen_first = current
        visible = moved[:, 2 * HEAD_DIM][None, :] == chunk_qtag[:, None]
        state = attend(
            state, chunk_q, moved[:, :HEAD_DIM], moved[:, HEAD_DIM : 2 * HEAD_DIM], visible
        )
        moved_index = (chunk_row - distance) * chunk_count + chunk_offsets
        seen_first = jnp.minimum(seen_first, first_of(moved[:, 2 * HEAD_DIM + 1], moved_index))
        return (state, seen_first)

    def cycle_turn(turn_index, loop_state):
        current, moved = loop_state
        following = passed_along(moved, "seq_hi", 1)
        return (visit_block(current, moved, turn_index + 1), following)

    reach_count = lo_count * hi_count // 2 * tok_count // chunk_count
    seen_first = first_of(chunk_qtag, chunk_row * chunk_count + chunk_offsets)
    moved = passed_along(ring_own, "seq_hi", 1)
    (softmax_state, seen_first), moved = lax.fori_loop(
        0, reach_count - 1, cycle_turn, ((softmax_state, seen_first), moved)
    )
    last_tags = moved[:, 2 * HEAD_DIM]
    row_parts = []
    part_rows = chunk_count // lo_count
    for part in range(lo_count):
        rows = slice(part * part_rows, (part + 1) * part_rows)
        keys = slice(part * part_rows, chunk_count)
        visible = last_tags[keys][None, :] == chunk_qtag[rows][:, None]
        row_parts.append(
            attend(
                tuple(s[rows] for s in softmax_state),
                chunk_q[rows],
                moved[keys, :HEAD_DIM],
                moved[keys, HEAD_DIM : 2 * HEAD_DIM],
                visible,
            )
        )
    softmax_state = tuple(jnp.concatenate(parts, axis=0) for parts in zip(*row_parts))
    last_index = (chunk_row - reach_count) * chunk_count + chunk_offsets
    first_tok = jnp.minimum(seen_first, first_of(moved[:, 2 * HEAD_DIM + 1], last_index))
    member = segment_ids[:, None] == jnp.arange(seg_count, dtype=jnp.int32)[None, :]
    position = tok_index - jnp.sum(jnp.where(member, first_tok[None, :], 0), axis=1)
    k_rot = rotate(key_proj, position, head_count, HEAD_DIM)
    row_peak, row_total, weighted = softmax_state
    chunk_attn = (weighted / row_total[:, None]).astype(jnp.bfloat16)
    back = lax.all_to_all(
        chunk_attn.reshape(lo_count, tok_count, HEAD_DIM), "seq_lo", 0, 0, tiled=True
    )
    attn = back.transpose(1, 0, 2).reshape(tok_count, feat_count)
    partial_value = jnp.dot(attn, out_weight, preferred_element_type=jnp.float32)
    feature_width = hidden.shape[1]
    tp_count = lax.axis_size("tp")
    pieces = (
        partial_value.astype(jnp.bfloat16)
        .reshape(tok_count, tp_count, feature_width)
        .transpose(1, 0, 2)
    )
    gathered = lax.all_to_all(pieces, "tp", 0, 0, tiled=True)
    own_sum = jnp.sum(gathered.astype(jnp.float32), axis=0)
    hidden_out = (hidden.astype(jnp.float32) + own_sum).astype(jnp.bfloat16)
    stream_wide = hidden_out.astype(jnp.float32)
    square_part = jnp.sum(stream_wide * stream_wide, axis=1)
    square_total = jnp.sum(
        lax.all_to_all(
            jnp.broadcast_to(square_part[None, :], (tp_count, tok_count)), "tp", 0, 0, tiled=True
        ),
        axis=0,
    )
    normed = (
        stream_wide
        * lax.rsqrt(square_total / D + norm_epsilon)[:, None]
        * norm_gain.astype(jnp.float32)[None, :]
    ).astype(jnp.bfloat16)
    pad_scale = pad_mask.astype(jnp.bfloat16)[:, None]
    page_count = tok_count // PAGE
    stacked = jnp.stack([k_rot * pad_scale, value_proj * pad_scale])
    stacked = stacked.reshape(2, page_count, PAGE, feat_count).transpose(1, 0, 2, 3)
    kv_pages = jnp.zeros_like(stacked).at[page_table].set(stacked)
    return (hidden_out, normed, kv_pages)


def solution(mesh):
    seq_count = mesh.shape["seq"]
    head_count = D // mesh.shape["tp"] // HEAD_DIM
    grouped = Mesh(
        mesh.devices.reshape(seq_count // head_count, head_count, mesh.shape["tp"]),
        ("seq_hi", "seq_lo", "tp"),
    )
    rows = ("seq_hi", "seq_lo")
    placed = (
        P(rows, "tp"),
        P(rows, "tp"),
        P(rows, "tp"),
        P(rows, "tp"),
        P("tp", None),
        P("tp"),
        P(rows),
        P(rows),
        P(rows),
    )
    return jax.shard_map(
        per_device,
        mesh=grouped,
        in_specs=placed,
        out_specs=(P(rows, "tp"), P(rows, "tp"), P(rows, None, None, "tp")),
        check_vma=False,
    )
```

```python
import math

import jax
import jax.numpy as jnp
from jax import lax
from jax.sharding import Mesh, PartitionSpec as P

D = 3072
HEAD_DIM = 96
PAGE = 128


far_index = 1073741824
masked_score = -1e30
norm_epsilon = 1e-05


def passed_along(block, axis, distance):
    devices = range(lax.axis_size(axis))
    route = [(i - distance, i) for i in devices if i - distance in devices]
    return lax.ppermute(block, axis, route)


def rotate(values_in, position, head_count, head_dim):
    count_rows = values_in.shape[0]
    half_dim = head_dim // 2
    frequency = jnp.exp(
        jnp.arange(half_dim, dtype=jnp.float32) * (-2.0 * math.log(10000.0) / head_dim)
    )
    angles = position.astype(jnp.float32)[:, None] * frequency[None, :]
    cosine = jnp.cos(angles)[:, None, :]
    sine_part = jnp.sin(angles)[:, None, :]
    as_float = values_in.astype(jnp.float32).reshape(count_rows, head_count, head_dim)
    lower_half = as_float[..., :half_dim]
    upper_half = as_float[..., half_dim:]
    rotated = jnp.concatenate(
        [
            lower_half * cosine - upper_half * sine_part,
            upper_half * cosine + lower_half * sine_part,
        ],
        axis=-1,
    )
    return rotated.reshape(count_rows, head_count * head_dim).astype(jnp.bfloat16)


def attend(softmax_state, query_heads, key_heads, val_heads, visible):
    row_peak, row_total, weighted = softmax_state
    factor = 1.0 / math.sqrt(HEAD_DIM)
    logits = (
        jnp.einsum("qd,kd->qk", query_heads, key_heads, preferred_element_type=jnp.float32)
        * factor
    )
    logits = jnp.where(visible, logits, masked_score)
    new_peak = jnp.maximum(row_peak, jnp.max(logits, axis=-1))
    rescale = jnp.exp(row_peak - new_peak)
    unnormed = jnp.where(visible, jnp.exp(logits - new_peak[..., None]), 0.0)
    row_total = row_total * rescale + jnp.sum(unnormed, axis=-1)
    weighted = weighted * rescale[..., None] + jnp.einsum(
        "qk,kd->qd", unnormed.astype(jnp.bfloat16), val_heads, preferred_element_type=jnp.float32
    )
    return (new_peak, row_total, weighted)


def per_device(
    query_proj,
    key_proj,
    value_proj,
    hidden,
    out_weight,
    norm_gain,
    segment_ids,
    pad_mask,
    page_table,
):
    tok_count = query_proj.shape[0]
    feat_count = query_proj.shape[1]
    head_count = feat_count // HEAD_DIM
    lo_count = lax.axis_size("seq_lo")
    hi_count = lax.axis_size("seq_hi")
    seg_count = lo_count * hi_count // 2
    device_row = lax.axis_index("seq_hi") * lo_count + lax.axis_index("seq_lo")
    tok_index = device_row * tok_count + jnp.arange(tok_count, dtype=jnp.int32)
    k_abs = rotate(key_proj, tok_index, head_count, HEAD_DIM)
    query_tag = segment_ids + 1
    key_tag = jnp.where(pad_mask == 1, segment_ids + 1, 0)
    seg_tags = jnp.arange(1, seg_count + 1, dtype=jnp.int32)

    def first_of(tag_values, index_values):
        hit = tag_values[:, None] == seg_tags[None, :].astype(tag_values.dtype)
        return jnp.min(jnp.where(hit, index_values[:, None], far_index), axis=0)

    tags = jnp.stack([key_tag, query_tag], axis=-1).astype(jnp.bfloat16)
    payload = jnp.concatenate(
        [
            query_proj.reshape(tok_count, head_count, HEAD_DIM),
            k_abs.reshape(tok_count, head_count, HEAD_DIM),
            value_proj.reshape(tok_count, head_count, HEAD_DIM),
            jnp.broadcast_to(tags[:, None, :], (tok_count, head_count, 2)),
        ],
        axis=-1,
    ).transpose(1, 0, 2)
    chunk = lax.all_to_all(payload, "seq_lo", 0, 0, tiled=True)
    chunk_count = lo_count * tok_count
    chunk = chunk.reshape(chunk_count, 3 * HEAD_DIM + 2)
    chunk_q = rotate(
        chunk[:, :HEAD_DIM],
        lax.axis_index("seq_hi") * chunk_count + jnp.arange(chunk_count, dtype=jnp.int32),
        1,
        HEAD_DIM,
    )
    chunk_k = chunk[:, HEAD_DIM : 2 * HEAD_DIM]
    chunk_v = chunk[:, 2 * HEAD_DIM : 3 * HEAD_DIM]
    chunk_ktag = chunk[:, 3 * HEAD_DIM]
    chunk_qtag = chunk[:, 3 * HEAD_DIM + 1]
    ring_own = chunk[:, HEAD_DIM : 3 * HEAD_DIM + 2]
    chunk_row = lax.axis_index("seq_hi")
    chunk_offsets = jnp.arange(chunk_count, dtype=jnp.int32)

    offsets = jnp.arange(chunk_count, dtype=jnp.int32)
    own_visible = (chunk_ktag[None, :] == chunk_qtag[:, None]) & (
        offsets[None, :] <= offsets[:, None]
    ) | (offsets[None, :] == offsets[:, None])
    softmax_state = (
        jnp.full((chunk_count,), masked_score, jnp.float32),
        jnp.zeros((chunk_count,), jnp.float32),
        jnp.zeros((chunk_count, HEAD_DIM), jnp.float32),
    )
    softmax_state = attend(softmax_state, chunk_q, chunk_k, chunk_v, own_visible)

    def visit_block(current, moved, distance):
        state, seen_first = current
        visible = moved[:, 2 * HEAD_DIM][None, :] == chunk_qtag[:, None]
        state = attend(
            state, chunk_q, moved[:, :HEAD_DIM], moved[:, HEAD_DIM : 2 * HEAD_DIM], visible
        )
        moved_index = (chunk_row - distance) * chunk_count + chunk_offsets
        seen_first = jnp.minimum(seen_first, first_of(moved[:, 2 * HEAD_DIM + 1], moved_index))
        return (state, seen_first)

    def cycle_turn(turn_index, loop_state):
        current, moved = loop_state
        following = passed_along(moved, "seq_hi", 1)
        return (visit_block(current, moved, turn_index + 1), following)

    reach_count = lo_count * hi_count // 2 * tok_count // chunk_count
    seen_first = first_of(chunk_qtag, chunk_row * chunk_count + chunk_offsets)
    moved = passed_along(ring_own, "seq_hi", 1)
    (softmax_state, seen_first), moved = lax.fori_loop(
        0, reach_count - 1, cycle_turn, ((softmax_state, seen_first), moved)
    )
    softmax_state, first_tok = visit_block((softmax_state, seen_first), moved, reach_count)
    member = segment_ids[:, None] == jnp.arange(seg_count, dtype=jnp.int32)[None, :]
    position = tok_index - jnp.sum(jnp.where(member, first_tok[None, :], 0), axis=1)
    k_rot = rotate(key_proj, position, head_count, HEAD_DIM)
    row_peak, row_total, weighted = softmax_state
    chunk_attn = (weighted / row_total[:, None]).astype(jnp.bfloat16)
    back = lax.all_to_all(
        chunk_attn.reshape(lo_count, tok_count, HEAD_DIM), "seq_lo", 0, 0, tiled=True
    )
    attn = back.transpose(1, 0, 2).reshape(tok_count, feat_count)
    partial_value = jnp.dot(attn, out_weight, preferred_element_type=jnp.float32)
    feature_width = hidden.shape[1]
    tp_count = lax.axis_size("tp")
    pieces = (
        partial_value.astype(jnp.bfloat16)
        .reshape(tok_count, tp_count, feature_width)
        .transpose(1, 0, 2)
    )
    gathered = lax.all_to_all(pieces, "tp", 0, 0, tiled=True)
    own_sum = jnp.sum(gathered.astype(jnp.float32), axis=0)
    hidden_out = (hidden.astype(jnp.float32) + own_sum).astype(jnp.bfloat16)
    stream_wide = hidden_out.astype(jnp.float32)
    square_part = jnp.sum(stream_wide * stream_wide, axis=1)
    square_total = jnp.sum(
        lax.all_to_all(
            jnp.broadcast_to(square_part[None, :], (tp_count, tok_count)), "tp", 0, 0, tiled=True
        ),
        axis=0,
    )
    normed = (
        stream_wide
        * lax.rsqrt(square_total / D + norm_epsilon)[:, None]
        * norm_gain.astype(jnp.float32)[None, :]
    ).astype(jnp.bfloat16)
    pad_scale = pad_mask.astype(jnp.bfloat16)[:, None]
    page_count = tok_count // PAGE
    stacked = jnp.stack([k_rot * pad_scale, value_proj * pad_scale])
    stacked = stacked.reshape(2, page_count, PAGE, feat_count).transpose(1, 0, 2, 3)
    kv_pages = jnp.zeros_like(stacked).at[page_table].set(stacked)
    return (hidden_out, normed, kv_pages)


def solution(mesh):
    seq_count = mesh.shape["seq"]
    head_count = D // mesh.shape["tp"] // HEAD_DIM
    grouped = Mesh(
        mesh.devices.reshape(seq_count // head_count, head_count, mesh.shape["tp"]),
        ("seq_hi", "seq_lo", "tp"),
    )
    rows = ("seq_hi", "seq_lo")
    placed = (
        P(rows, "tp"),
        P(rows, "tp"),
        P(rows, "tp"),
        P(rows, "tp"),
        P("tp", None),
        P("tp"),
        P(rows),
        P(rows),
        P(rows),
    )
    return jax.shard_map(
        per_device,
        mesh=grouped,
        in_specs=placed,
        out_specs=(P(rows, "tp"), P(rows, "tp"), P(rows, None, None, "tp")),
        check_vma=False,
    )
```
